32 devices in a mesh: brick: 4 (over z), batch: 8 (over y, x, core).
Axes of the slice: x: 2, y: 2, z: 4, core: 2. Of those that a mesh axis runs over, the one named last changes fastest.
Arguments:
- coarse: bfloat16 [8, 4, 4, 8, 1024], P('batch', 'brick'), may hold values from -6 to 6
- coarse_mask: int32 [8, 4, 256], P('batch', 'brick'), may hold values 0 or 1
- skip: bfloat16 [8, 4, 8, 16, 1024], P('batch', 'brick'), may hold values from -6 to 6
- fine_mask: int32 [8, 4, 2048], P('batch', 'brick'), may hold values 0 or 1
- up_weight: bfloat16 [27, 64, 128], replicated, may hold values from -0.25 to 0.25
- fine_grad: bfloat16 [8, 4, 8, 16, 1024], P('batch', 'brick'), may hold values from -6 to 6
Outputs:
- fine_out: bfloat16 [8, 4, 8, 16, 1024], P('batch', 'brick')
- coarse_grad: bfloat16 [8, 4, 4, 8, 1024], P('batch', 'brick')
- weight_grad: float32 [27, 64, 128], replicated
The draws below stay inside these ranges and needn't reach their ends.
All inputs are finite; a program needn't handle non-finite values. No bound on the sum of `coarse_mask` or of `fine_mask` on one device may be relied on, other than what follows from the above.
Results may differ from the reference program's by a relative error of at most 0.0035.
Values may be sent and summed in bfloat16 or wider, within the bound.
No kernel may reach another device: no remote copies, remote signals or barrier semaphores. Data moves between devices by JAX's collectives and lax.ppermute only.
A program may use at most 64 MiB of HBM per device.

```python
import math
import jax
import jax.numpy as jnp
from jax import lax

CH_FINE = 64
CH_COARSE = 128
FX = 8
FY = 16
FZ = 16
CX = 4
CY = 8
CZ = 8
REGIONS = 4
SCENES = 8


def set_ends(array, own_key, smallest, largest):
    shape = array.shape
    spot = [jax.random.randint(jax.random.fold_in(own_key, axis), (), 0, shape[axis]) for axis in range(len(shape))]
    array = array.at[tuple(spot)].set(smallest)
    longest = shape.index(max(shape))
    spot[longest] = (spot[longest] + 1) % shape[longest]
    return array.at[tuple(spot)].set(largest)


def levels(rng, shape, shards, smallest, top_value):
    gain = 1.0
    for position, blocks in shards:
        heights = jax.random.uniform(jax.random.fold_in(jax.random.fold_in(rng, 6), position), (blocks,), jnp.float32, smallest / len(shards), top_value / len(shards))
        gain = gain * jnp.repeat(jnp.exp(heights), shape[position] // blocks).reshape((-1,) + (1,) * (len(shape) - 1 - position))
    return gain


def scatter_about(rng, dims, scale, reach, shards=(), dtype=jnp.bfloat16):
    values = jax.random.normal(rng, dims, jnp.float32) * scale
    if len(shards) > 0:
        values = levels(rng, dims, shards, -0.22, 0.18) * values
    return jnp.clip(values, min=-reach, max=reach).astype(dtype)


def setup_inputs(seed: int = 0) -> dict:
    streams_of = jax.random.split(jax.random.key(seed), 7)
    return {
        "coarse": scatter_about(streams_of[0], (SCENES, REGIONS, CX, CY, CZ * CH_COARSE), 1.0, 6.0, ((0, 8), (1, 4))),
        "coarse_mask": set_ends((jax.random.randint(streams_of[1], (SCENES, REGIONS, CX * CY * CZ), 0, 5) < 4).astype(jnp.int32), jax.random.fold_in(streams_of[1], 1), 0, 1),
        "skip": scatter_about(streams_of[2], (SCENES, REGIONS, FX, FY, FZ * CH_FINE), 1.0, 6.0, ((0, 8), (1, 4))),
        "fine_mask": set_ends((jax.random.randint(streams_of[3], (SCENES, REGIONS, FX * FY * FZ), 0, 4) < 3).astype(jnp.int32), jax.random.fold_in(streams_of[3], 1), 0, 1),
        "up_weight": scatter_about(streams_of[4], (27, CH_FINE, CH_COARSE), (4 * CH_COARSE) ** -0.5, 0.25),
        "fine_grad": scatter_about(streams_of[5], (SCENES, REGIONS, FX, FY, FZ * CH_FINE), 1.0, 6.0, ((0, 8), (1, 4))),
    }


EVEN_TAPS = ((1, 0),)
ODD_TAPS = ((2, 0), (0, 1))

def tap_pairs(parity):
    if parity == 0:
        return EVEN_TAPS
    return ODD_TAPS

def spread(padded, weight):
    counts = (padded.shape[0] - 1, padded.shape[1] - 1, padded.shape[2] - 1)
    outputs = weight.shape[1]
    parts = []
    for parity_x in range(2):
        for parity_y in range(2):
            for parity_z in range(2):
                total = jnp.zeros(counts + (outputs,), jnp.float32)
                for tap_x, start_x in tap_pairs(parity_x):
                    for tap_y, start_y in tap_pairs(parity_y):
                        for tap_z, start_z in tap_pairs(parity_z):
                            window = padded[start_x:start_x + counts[0], start_y:start_y + counts[1], start_z:start_z + counts[2]]
                            total = total + jnp.einsum('abci,oi->abco', window, weight[9 * tap_x + 3 * tap_y + tap_z], preferred_element_type=jnp.float32)
                parts.append(total)
    stacked = jnp.stack(parts).reshape((2, 2, 2) + counts + (outputs,))
    return stacked.transpose(3, 0, 4, 1, 5, 2, 6).reshape(2 * counts[0], 2 * counts[1], 2 * counts[2], outputs)

def pick(field, tap, count, axis):
    return lax.slice_in_dim(field, tap, tap + 2 * count - 1, 2, axis)

def adjoint(widened, masked, weight):
    counts = masked.shape[:3]
    back = jnp.zeros(masked.shape, jnp.float32)
    grads = []
    for tap_x in range(3):
        along_x = pick(widened, tap_x, counts[0], 0)
        for tap_y in range(3):
            along_y = pick(along_x, tap_y, counts[1], 1)
            for tap_z in range(3):
                chosen = pick(along_y, tap_z, counts[2], 2)
                index = 9 * tap_x + 3 * tap_y + tap_z
                back = back + jnp.einsum('abco,oi->abci', chosen, weight[index], preferred_element_type=jnp.float32)
                grads.append(jnp.einsum('abco,abci->oi', chosen, masked, preferred_element_type=jnp.float32))
    return (back, jnp.stack(grads))

def assemble(blocks, channels):
    regions, size_x, size_y, merged = blocks.shape
    size_z = merged // channels
    grid_x = regions // 4
    shaped = blocks.reshape(grid_x, 2, 2, size_x, size_y, size_z, channels)
    return shaped.transpose(0, 3, 1, 4, 2, 5, 6).reshape(grid_x * size_x, 2 * size_y, 2 * size_z, channels)

def split_up(scene, size_x, size_y, size_z):
    grid_x = scene.shape[0] // size_x
    channels = scene.shape[3]
    shaped = scene.reshape(grid_x, size_x, 2, size_y, 2, size_z, channels)
    return shaped.transpose(0, 2, 4, 1, 3, 5, 6).reshape(grid_x * 4, size_x, size_y, size_z * channels)

def reference(coarse, coarse_mask, skip, fine_mask, up_weight, fine_grad):
    weight = up_weight.astype(jnp.float32)

    def one_scene(items):
        coarse_one, coarse_keep, skip_one, fine_keep, grad_one = items
        keep_coarse = assemble(coarse_keep.reshape(REGIONS, CX, CY, CZ), 1).astype(jnp.float32)
        masked = assemble(coarse_one, CH_COARSE).astype(jnp.float32) * keep_coarse
        up = spread(jnp.pad(masked, ((0, 1), (0, 1), (0, 1), (0, 0))), weight)
        keep_fine = assemble(fine_keep.reshape(REGIONS, FX, FY, FZ), 1).astype(jnp.float32)
        fine = (keep_fine * (assemble(skip_one, CH_FINE).astype(jnp.float32) + up)).astype(jnp.bfloat16)
        cotangent = keep_fine * assemble(grad_one, CH_FINE).astype(jnp.float32)
        widened = jnp.pad(cotangent, ((1, 0), (1, 0), (1, 0), (0, 0)))
        back, grads = adjoint(widened, masked, weight)
        coarse_out = (keep_coarse * back).astype(jnp.bfloat16)
        return (split_up(fine, FX, FY, FZ), split_up(coarse_out, CX, CY, CZ), grads)
    fine_all, coarse_all, grads_all = lax.map(one_scene, (coarse, coarse_mask, skip, fine_mask, fine_grad))
    scale = 1.0 / math.sqrt(SCENES * REGIONS * CX * CY * CZ)
    return (fine_all, coarse_all, lax.optimization_barrier(jnp.sum(grads_all, axis=0)) * scale)
```

```python
import math

import jax
import jax.numpy as jnp
from jax import lax
from jax.sharding import PartitionSpec as P

OFFSETS = tuple((dx, dy, dz) for dx in range(2) for dy in range(2) for dz in range(2))
DIRECTIONS = OFFSETS[1:]
AXES = ("brick", "batch")


def region_of(rank):
    return (rank // 4, rank // 2 % 2, rank % 2)


def neighbour_pairs(regions, direction, sign):
    grid = (regions // 4, 2, 2)
    pairs = []
    for dst in range(regions):
        spot = region_of(dst)
        src = tuple(spot[a] + sign * direction[a] for a in range(3))
        if all(0 <= src[a] < grid[a] for a in range(3)):
            pairs.append((4 * src[0] + 2 * src[1] + src[2], dst))
    return pairs


def exchange(piece, regions, direction, sign):
    pairs = neighbour_pairs(regions, direction, sign)
    if not pairs:
        return jnp.zeros_like(piece)
    return lax.ppermute(piece, "brick", pairs)


def forward_tap(d, p):
    k = p + 1 - 2 * d
    return k if 0 <= k <= 2 else None


def forward_weight(up_weight):
    zero = jnp.zeros(up_weight.shape[1:], up_weight.dtype)
    rows = []
    for d in OFFSETS:
        row = []
        for p in OFFSETS:
            taps = [forward_tap(d[a], p[a]) for a in range(3)]
            if any(t is None for t in taps):
                row.append(zero)
            else:
                row.append(up_weight[9 * taps[0] + 3 * taps[1] + taps[2]])
        rows.append(jnp.stack(row))
    return jnp.stack(rows)


def all_reduce(grads):
    devices = lax.axis_size("brick") * lax.axis_size("batch")
    flat = grads.reshape(-1)
    size = flat.shape[0]
    chunk = -(-size // devices)
    flat = jnp.pad(flat, (0, chunk * devices - size))
    parts = lax.all_to_all(flat.reshape(devices, chunk), AXES, 0, 0, tiled=True)
    return parts.sum(axis=0), (devices, chunk, size)


def all_spread(reduced, plan):
    devices, chunk, size = plan
    spread = jnp.broadcast_to(reduced[None], (devices, chunk))
    whole = lax.all_to_all(spread, AXES, 0, 0, tiled=True)
    return whole.reshape(-1)[:size]


def body(coarse, coarse_mask, skip, fine_mask, up_weight, fine_grad):
    regions = lax.axis_size("brick")
    size_x, size_y, merged = coarse.shape[2:]
    channels_out = up_weight.shape[1]
    channels_in = up_weight.shape[2]
    size_z = merged // channels_in
    fine_x, fine_y, fine_merged = skip.shape[2:]
    fine_z = fine_merged // channels_out
    counts = (size_x, size_y, size_z)

    coarse_keep = coarse_mask.reshape(size_x, size_y, size_z, 1).astype(jnp.bfloat16)
    masked = coarse.reshape(size_x, size_y, size_z, channels_in) * coarse_keep
    fine_keep = fine_mask.reshape(fine_x, fine_y, fine_z, 1)
    cotangent = fine_grad.reshape(fine_x, fine_y, fine_z, channels_out) * fine_keep.astype(
        jnp.bfloat16
    )

    widened = jnp.pad(cotangent, ((1, 1), (1, 1), (1, 1), (0, 0)))
    for direction in DIRECTIONS:
        source = tuple(slice(-1, None) if flag else slice(None) for flag in direction)
        got = exchange(cotangent[source], regions, direction, -1)
        target = tuple(
            slice(0, 1) if flag else slice(1, 1 + cotangent.shape[a])
            for a, flag in enumerate(direction)
        )
        widened = widened.at[target].set(got)
    extended = jnp.pad(masked, ((0, 1), (0, 1), (0, 1), (0, 0)))
    for direction in DIRECTIONS:
        source = tuple(slice(0, 1) if flag else slice(None) for flag in direction)
        got = exchange(masked[source], regions, direction, 1)
        target = tuple(
            slice(counts[a], counts[a] + 1) if flag else slice(0, counts[a])
            for a, flag in enumerate(direction)
        )
        extended = extended.at[target].set(got)

    paired = widened.reshape(size_x + 1, 2, size_y + 1, 2, size_z + 1, 2, channels_out)
    windows = []
    for kx in range(3):
        for ky in range(3):
            for kz in range(3):
                index = []
                for k, count in zip((kx, ky, kz), counts):
                    start = 1 if k == 2 else 0
                    index += [slice(start, start + count), 0 if k != 1 else 1]
                windows.append(paired[tuple(index)])
    gathered = jnp.stack(windows)
    grads = jnp.einsum(
        "kabco,abci->koi", gathered, masked, preferred_element_type=jnp.float32
    )
    reduced, plan = all_reduce(grads)

    back = jnp.einsum(
        "kabco,koi->abci", gathered, up_weight, preferred_element_type=jnp.float32
    )
    coarse_grad = (
        (back * coarse_keep.astype(jnp.float32)).astype(jnp.bfloat16).reshape(coarse.shape)
    )

    shifted = jnp.stack(
        [
            extended[dx : dx + size_x, dy : dy + size_y, dz : dz + size_z]
            for dx, dy, dz in OFFSETS
        ]
    )
    parities = jnp.einsum(
        "dabci,dpoi->abcpo",
        shifted,
        forward_weight(up_weight),
        preferred_element_type=jnp.float32,
    )
    up = (
        parities.reshape(size_x, size_y, size_z, 2, 2, 2, channels_out)
        .transpose(0, 3, 1, 4, 2, 5, 6)
        .reshape(fine_x, fine_y, fine_z, channels_out)
    )
    fine = fine_keep.astype(jnp.float32) * (
        skip.reshape(fine_x, fine_y, fine_z, channels_out).astype(jnp.float32) + up
    )
    fine_out = fine.astype(jnp.bfloat16).reshape(skip.shape)

    scale = 1.0 / math.sqrt(regions * lax.axis_size("batch") * size_x * size_y * size_z)
    weight_grad = all_spread(reduced * scale, plan).reshape(grads.shape)
    return (fine_out, coarse_grad, weight_grad)


def solution(mesh):
    in_specs = (
        P("batch", "brick", None, None, None),
        P("batch", "brick", None),
        P("batch", "brick", None, None, None),
        P("batch", "brick", None),
        P(),
        P("batch", "brick", None, None, None),
    )
    out_specs = (P("batch", "brick", None, None, None), P("batch", "brick", None, None, None), P())
    return jax.shard_map(body, mesh=mesh, in_specs=in_specs, out_specs=out_specs, check_vma=False)
```

```python
import math

import jax
import jax.numpy as jnp
from jax import lax
from jax.sharding import PartitionSpec as P

OFFSETS = tuple((dx, dy, dz) for dx in range(2) for dy in range(2) for dz in range(2))
DIRECTIONS = OFFSETS[1:]
AXES = ("brick", "batch")


def region_of(rank):
    return (rank // 4, rank // 2 % 2, rank % 2)


def neighbour_pairs(regions, direction, sign):
    grid = (regions // 4, 2, 2)
    pairs = []
    for dst in range(regions):
        spot = region_of(dst)
        src = tuple(spot[a] + sign * direction[a] for a in range(3))
        if all(0 <= src[a] < grid[a] for a in range(3)):
            pairs.append((4 * src[0] + 2 * src[1] + src[2], dst))
    return pairs


def exchange(piece, regions, direction, sign):
    pairs = neighbour_pairs(regions, direction, sign)
    if not pairs:
        return jnp.zeros_like(piece)
    return lax.ppermute(piece, "brick", pairs)


def forward_weight(up_weight):
    channels = up_weight.shape[1:]
    taps = jnp.pad(up_weight.reshape((3, 3, 3) + channels), ((0, 1), (0, 1), (0, 1), (0, 0), (0, 0)))
    for axis in range(3):
        taps = jnp.roll(taps, -1, axis=axis)
    return taps.reshape((2, 2, 2, 2, 2, 2) + channels)


def all_reduce(grads):
    devices = lax.axis_size("brick") * lax.axis_size("batch")
    flat = grads.reshape(-1)
    size = flat.shape[0]
    chunk = -(-size // devices)
    flat = jnp.pad(flat, (0, chunk * devices - size))
    parts = lax.all_to_all(flat.reshape(devices, chunk), AXES, 0, 0, tiled=True)
    return parts.sum(axis=0), (devices, chunk, size)


def all_spread(reduced, plan):
    devices, chunk, size = plan
    spread = jnp.broadcast_to(reduced[None], (devices, chunk))
    whole = lax.all_to_all(spread, AXES, 0, 0, tiled=True)
    return whole.reshape(-1)[:size]


def body(coarse, coarse_mask, skip, fine_mask, up_weight, fine_grad):
    regions = lax.axis_size("brick")
    size_x, size_y, merged = coarse.shape[2:]
    channels_out = up_weight.shape[1]
    channels_in = up_weight.shape[2]
    size_z = merged // channels_in
    fine_x, fine_y, fine_merged = skip.shape[2:]
    fine_z = fine_merged // channels_out
    counts = (size_x, size_y, size_z)

    coarse_keep = coarse_mask.reshape(size_x, size_y, size_z, 1).astype(jnp.bfloat16)
    masked = coarse.reshape(size_x, size_y, size_z, channels_in) * coarse_keep
    fine_keep = fine_mask.reshape(fine_x, fine_y, fine_z, 1)
    cotangent = fine_grad.reshape(fine_x, fine_y, fine_z, channels_out) * fine_keep.astype(
        jnp.bfloat16
    )

    widened = jnp.pad(cotangent, ((1, 1), (1, 1), (1, 1), (0, 0)))
    for direction in DIRECTIONS:
        source = tuple(slice(-1, None) if flag else slice(None) for flag in direction)
        got = exchange(cotangent[source], regions, direction, -1)
        target = tuple(
            slice(0, 1) if flag else slice(1, 1 + cotangent.shape[a])
            for a, flag in enumerate(direction)
        )
        widened = widened.at[target].set(got)
    paired = widened.reshape(size_x + 1, 2, size_y + 1, 2, size_z + 1, 2, channels_out)
    windows = []
    for kx in range(3):
        for ky in range(3):
            for kz in range(3):
                index = []
                for k, count in zip((kx, ky, kz), counts):
                    start = 1 if k == 2 else 0
                    index += [slice(start, start + count), 0 if k != 1 else 1]
                windows.append(paired[tuple(index)])
    gathered = jnp.stack(windows)
    grads = jnp.einsum(
        "kabco,abci->koi", gathered, masked, preferred_element_type=jnp.float32
    )
    reduced, plan = all_reduce(grads)
    reduced, masked_late, weight_late = lax.optimization_barrier((reduced, masked, up_weight))

    back = jnp.einsum(
        "kabco,koi->abci", gathered, up_weight, preferred_element_type=jnp.float32
    )
    coarse_grad = (
        (back * coarse_keep.astype(jnp.float32)).astype(jnp.bfloat16).reshape(coarse.shape)
    )

    extended = jnp.pad(masked_late, ((0, 1), (0, 1), (0, 1), (0, 0)))
    for direction in DIRECTIONS:
        source = tuple(slice(0, 1) if flag else slice(None) for flag in direction)
        got = exchange(masked_late[source], regions, direction, 1)
        target = tuple(
            slice(counts[a], counts[a] + 1) if flag else slice(0, counts[a])
            for a, flag in enumerate(direction)
        )
        extended = extended.at[target].set(got)

    shifted = jnp.stack(
        [
            extended[dx : dx + size_x, dy : dy + size_y, dz : dz + size_z]
            for dx, dy, dz in OFFSETS
        ]
    ).reshape((2, 2, 2, size_x, size_y, size_z, channels_in))
    parities = jnp.einsum(
        "xyzabci,xpyqzroi->apbqcro",
        shifted,
        forward_weight(weight_late),
        preferred_element_type=jnp.float32,
    )
    up = parities.reshape(fine_x, fine_y, fine_z, channels_out)
    fine = fine_keep.astype(jnp.float32) * (
        skip.reshape(fine_x, fine_y, fine_z, channels_out).astype(jnp.float32) + up
    )
    fine_out = fine.astype(jnp.bfloat16).reshape(skip.shape)

    scale = 1.0 / math.sqrt(regions * lax.axis_size("batch") * size_x * size_y * size_z)
    weight_grad = all_spread(reduced * scale, plan).reshape(grads.shape)
    return (fine_out, coarse_grad, weight_grad)


def solution(mesh):
    in_specs = (
        P("batch", "brick", None, None, None),
        P("batch", "brick", None),
        P("batch", "brick", None, None, None),
        P("batch", "brick", None),
        P(),
        P("batch", "brick", None, None, None),
    )
    out_specs = (P("batch", "brick", None, None, None), P("batch", "brick", None, None, None), P())
    return jax.shard_map(body, mesh=mesh, in_specs=in_specs, out_specs=out_specs, check_vma=False)
```

```python
import math

import jax
import jax.numpy as jnp
from jax import lax
from jax.sharding import PartitionSpec as P

OFFSETS = tuple((dx, dy, dz) for dx in range(2) for dy in range(2) for dz in range(2))
DIRECTIONS = OFFSETS[1:]
AXES = ("brick", "batch")


def region_of(rank):
    return (rank // 4, rank // 2 % 2, rank % 2)


def neighbour_pairs(regions, direction, sign):
    grid = (regions // 4, 2, 2)
    pairs = []
    for dst in range(regions):
        spot = region_of(dst)
        src = tuple(spot[a] + sign * direction[a] for a in range(3))
        if all(0 <= src[a] < grid[a] for a in range(3)):
            pairs.append((4 * src[0] + 2 * src[1] + src[2], dst))
    return pairs


def exchange(piece, regions, direction, sign):
    pairs = neighbour_pairs(regions, direction, sign)
    if not pairs:
        return jnp.zeros_like(piece)
    return lax.ppermute(piece, "brick", pairs)


def forward_weight(up_weight):
    channels = up_weight.shape[1:]
    taps = jnp.pad(up_weight.reshape((3, 3, 3) + channels), ((0, 1), (0, 1), (0, 1), (0, 0), (0, 0)))
    for axis in range(3):
        taps = jnp.roll(taps, -1, axis=axis)
    return taps.reshape((2, 2, 2, 2, 2, 2) + channels)


def all_reduce(grads):
    devices = lax.axis_size("brick") * lax.axis_size("batch")
    flat = grads.reshape(-1)
    size = flat.shape[0]
    chunk = -(-size // devices)
    flat = jnp.pad(flat, (0, chunk * devices - size))
    parts = lax.all_to_all(flat.reshape(devices, chunk), AXES, 0, 0, tiled=True)
    return parts.sum(axis=0), (devices, chunk, size)


def all_spread(reduced, plan):
    devices, chunk, size = plan
    spread = jnp.broadcast_to(reduced[None], (devices, chunk))
    whole = lax.all_to_all(spread, AXES, 0, 0, tiled=True)
    return whole.reshape(-1)[:size]


def body(coarse, coarse_mask, skip, fine_mask, up_weight, fine_grad):
    regions = lax.axis_size("brick")
    size_x, size_y, merged = coarse.shape[2:]
    channels_out = up_weight.shape[1]
    channels_in = up_weight.shape[2]
    size_z = merged // channels_in
    fine_x, fine_y, fine_merged = skip.shape[2:]
    fine_z = fine_merged // channels_out
    counts = (size_x, size_y, size_z)

    coarse_keep = coarse_mask.reshape(size_x, size_y, size_z, 1).astype(jnp.bfloat16)
    masked = coarse.reshape(size_x, size_y, size_z, channels_in) * coarse_keep
    fine_keep = fine_mask.reshape(fine_x, fine_y, fine_z, 1)
    cotangent = fine_grad.reshape(fine_x, fine_y, fine_z, channels_out) * fine_keep.astype(
        jnp.bfloat16
    )

    widened = jnp.pad(cotangent, ((1, 1), (1, 1), (1, 1), (0, 0)))
    for direction in DIRECTIONS:
        source = tuple(slice(-1, None) if flag else slice(None) for flag in direction)
        got = exchange(cotangent[source], regions, direction, -1)
        target = tuple(
            slice(0, 1) if flag else slice(1, 1 + cotangent.shape[a])
            for a, flag in enumerate(direction)
        )
        widened = widened.at[target].set(got)
    paired = widened.reshape(size_x + 1, 2, size_y + 1, 2, size_z + 1, 2, channels_out)
    windows = []
    for kx in range(3):
        for ky in range(3):
            for kz in range(3):
                index = []
                for k, count in zip((kx, ky, kz), counts):
                    start = 1 if k == 2 else 0
                    index += [slice(start, start + count), 0 if k != 1 else 1]
                windows.append(paired[tuple(index)])
    gathered = jnp.stack(windows)
    grads = jnp.einsum(
        "kabco,abci->koi", gathered, masked, preferred_element_type=jnp.float32
    )
    grads, masked_late, weight_late = lax.optimization_barrier((grads, masked, up_weight))
    reduced, plan = all_reduce(grads)

    back = jnp.einsum(
        "kabco,koi->abci", gathered, up_weight, preferred_element_type=jnp.float32
    )
    coarse_grad = (
        (back * coarse_keep.astype(jnp.float32)).astype(jnp.bfloat16).reshape(coarse.shape)
    )

    extended = jnp.pad(masked_late, ((0, 1), (0, 1), (0, 1), (0, 0)))
    for direction in DIRECTIONS:
        source = tuple(slice(0, 1) if flag else slice(None) for flag in direction)
        got = exchange(masked_late[source], regions, direction, 1)
        target = tuple(
            slice(counts[a], counts[a] + 1) if flag else slice(0, counts[a])
            for a, flag in enumerate(direction)
        )
        extended = extended.at[target].set(got)

    shifted = jnp.stack(
        [
            extended[dx : dx + size_x, dy : dy + size_y, dz : dz + size_z]
            for dx, dy, dz in OFFSETS
        ]
    ).reshape((2, 2, 2, size_x, size_y, size_z, channels_in))
    parities = jnp.einsum(
        "xyzabci,xpyqzroi->apbqcro",
        shifted,
        forward_weight(weight_late),
        preferred_element_type=jnp.float32,
    )
    up = parities.reshape(fine_x, fine_y, fine_z, channels_out)
    fine = fine_keep.astype(jnp.float32) * (
        skip.reshape(fine_x, fine_y, fine_z, channels_out).astype(jnp.float32) + up
    )
    fine_out = fine.astype(jnp.bfloat16).reshape(skip.shape)

    scale = 1.0 / math.sqrt(regions * lax.axis_size("batch") * size_x * size_y * size_z)
    weight_grad = all_spread(reduced * scale, plan).reshape(grads.shape)
    return (fine_out, coarse_grad, weight_grad)


def solution(mesh):
    in_specs = (
        P("batch", "brick", None, None, None),
        P("batch", "brick", None),
        P("batch", "brick", None, None, None),
        P("batch", "brick", None),
        P(),
        P("batch", "brick", None, None, None),
    )
    out_specs = (P("batch", "brick", None, None, None), P("batch", "brick", None, None, None), P())
    return jax.shard_map(body, mesh=mesh, in_specs=in_specs, out_specs=out_specs, check_vma=False)
```

```python
import math

import jax
import jax.numpy as jnp
from jax import lax
from jax.sharding import Mesh, PartitionSpec as P

OFFSETS = tuple((dx, dy, dz) for dx in range(2) for dy in range(2) for dz in range(2))
DIRECTIONS = OFFSETS[1:]
BATCH = ("chip", "core")
OTHERS = ("brick", "chip")


def region_of(rank):
    return (rank // 4, rank // 2 % 2, rank % 2)


def neighbour_pairs(regions, direction, sign):
    grid = (regions // 4, 2, 2)
    pairs = []
    for dst in range(regions):
        spot = region_of(dst)
        src = tuple(spot[a] + sign * direction[a] for a in range(3))
        if all(0 <= src[a] < grid[a] for a in range(3)):
            pairs.append((4 * src[0] + 2 * src[1] + src[2], dst))
    return pairs


def exchange(piece, regions, direction, sign):
    pairs = neighbour_pairs(regions, direction, sign)
    if not pairs:
        return jnp.zeros_like(piece)
    return lax.ppermute(piece, "brick", pairs)


def forward_weight(up_weight):
    channels = up_weight.shape[1:]
    taps = jnp.pad(up_weight.reshape((3, 3, 3) + channels), ((0, 1), (0, 1), (0, 1), (0, 0), (0, 0)))
    for axis in range(3):
        taps = jnp.roll(taps, -1, axis=axis)
    return taps.reshape((2, 2, 2, 2, 2, 2) + channels)


def all_reduce(grads):
    devices = lax.axis_size("brick") * lax.axis_size("chip")
    flat = grads.reshape(-1)
    size = flat.shape[0]
    chunk = -(-size // (2 * devices))
    flat = jnp.pad(flat, (0, 2 * chunk * devices - size)).reshape(2, devices * chunk)
    core = lax.axis_index("core")
    got = lax.ppermute(jnp.where(core == 0, flat[1], flat[0]), "core", [(0, 1), (1, 0)])
    half = jnp.where(core == 0, flat[0], flat[1]) + got
    parts = lax.all_to_all(half.reshape(devices, chunk), OTHERS, 0, 0, tiled=True)
    return parts.sum(axis=0), (devices, chunk, size)


def all_spread(reduced, plan):
    devices, chunk, size = plan
    spread = jnp.broadcast_to(reduced[None], (devices, chunk))
    half = lax.all_to_all(spread, OTHERS, 0, 0, tiled=True).reshape(-1)
    other = lax.ppermute(half, "core", [(0, 1), (1, 0)])
    core = lax.axis_index("core")
    whole = jnp.where(
        core == 0, jnp.concatenate([half, other]), jnp.concatenate([other, half])
    )
    return whole[:size]


def body(coarse, coarse_mask, skip, fine_mask, up_weight, fine_grad):
    regions = lax.axis_size("brick")
    size_x, size_y, merged = coarse.shape[2:]
    channels_out = up_weight.shape[1]
    channels_in = up_weight.shape[2]
    size_z = merged // channels_in
    fine_x, fine_y, fine_merged = skip.shape[2:]
    fine_z = fine_merged // channels_out
    counts = (size_x, size_y, size_z)

    coarse_keep = coarse_mask.reshape(size_x, size_y, size_z, 1).astype(jnp.bfloat16)
    masked = coarse.reshape(size_x, size_y, size_z, channels_in) * coarse_keep
    fine_keep = fine_mask.reshape(fine_x, fine_y, fine_z, 1)
    cotangent = fine_grad.reshape(fine_x, fine_y, fine_z, channels_out) * fine_keep.astype(
        jnp.bfloat16
    )

    widened = jnp.pad(cotangent, ((1, 1), (1, 1), (1, 1), (0, 0)))
    for direction in DIRECTIONS:
        source = tuple(slice(-1, None) if flag else slice(None) for flag in direction)
        got = exchange(cotangent[source], regions, direction, -1)
        target = tuple(
            slice(0, 1) if flag else slice(1, 1 + cotangent.shape[a])
            for a, flag in enumerate(direction)
        )
        widened = widened.at[target].set(got)
    paired = widened.reshape(size_x + 1, 2, size_y + 1, 2, size_z + 1, 2, channels_out)
    windows = []
    for kx in range(3):
        for ky in range(3):
            for kz in range(3):
                index = []
                for k, count in zip((kx, ky, kz), counts):
                    start = 1 if k == 2 else 0
                    index += [slice(start, start + count), 0 if k != 1 else 1]
                windows.append(paired[tuple(index)])
    gathered = jnp.stack(windows)
    grads = jnp.einsum(
        "kabco,abci->koi", gathered, masked, preferred_element_type=jnp.float32
    )
    grads, masked_late, weight_late = lax.optimization_barrier((grads, masked, up_weight))
    reduced, plan = all_reduce(grads)

    back = jnp.einsum(
        "kabco,koi->abci", gathered, up_weight, preferred_element_type=jnp.float32
    )
    coarse_grad = (
        (back * coarse_keep.astype(jnp.float32)).astype(jnp.bfloat16).reshape(coarse.shape)
    )

    extended = jnp.pad(masked_late, ((0, 1), (0, 1), (0, 1), (0, 0)))
    for direction in DIRECTIONS:
        source = tuple(slice(0, 1) if flag else slice(None) for flag in direction)
        got = exchange(masked_late[source], regions, direction, 1)
        target = tuple(
            slice(counts[a], counts[a] + 1) if flag else slice(0, counts[a])
            for a, flag in enumerate(direction)
        )
        extended = extended.at[target].set(got)

    shifted = jnp.stack(
        [
            extended[dx : dx + size_x, dy : dy + size_y, dz : dz + size_z]
            for dx, dy, dz in OFFSETS
        ]
    ).reshape((2, 2, 2, size_x, size_y, size_z, channels_in))
    parities = jnp.einsum(
        "xyzabci,xpyqzroi->apbqcro",
        shifted,
        forward_weight(weight_late),
        preferred_element_type=jnp.float32,
    )
    up = parities.reshape(fine_x, fine_y, fine_z, channels_out)
    fine = fine_keep.astype(jnp.float32) * (
        skip.reshape(fine_x, fine_y, fine_z, channels_out).astype(jnp.float32) + up
    )
    fine_out = fine.astype(jnp.bfloat16).reshape(skip.shape)

    scale = 1.0 / math.sqrt(regions * lax.axis_size("chip") * lax.axis_size("core") * size_x * size_y * size_z)
    weight_grad = all_spread(reduced * scale, plan).reshape(grads.shape)
    return (fine_out, coarse_grad, weight_grad)


def solution(mesh):
    brick, batch = mesh.shape["brick"], mesh.shape["batch"]
    pairs = Mesh(
        mesh.devices.reshape(brick, batch // 2, 2), ("brick", "chip", "core")
    )
    in_specs = (
        P(BATCH, "brick", None, None, None),
        P(BATCH, "brick", None),
        P(BATCH, "brick", None, None, None),
        P(BATCH, "brick", None),
        P(),
        P(BATCH, "brick", None, None, None),
    )
    out_specs = (P(BATCH, "brick", None, None, None), P(BATCH, "brick", None, None, None), P())
    return jax.shard_map(body, mesh=pairs, in_specs=in_specs, out_specs=out_specs, check_vma=False)
```

```python
import math

import jax
import jax.numpy as jnp
from jax import lax
from jax.sharding import Mesh, PartitionSpec as P

OFFSETS = tuple((dx, dy, dz) for dx in range(2) for dy in range(2) for dz in range(2))
DIRECTIONS = OFFSETS[1:]
BATCH = ("chip", "core")
OTHERS = ("brick", "chip")


def region_of(rank):
    return (rank // 4, rank // 2 % 2, rank % 2)


def neighbour_pairs(regions, direction, sign):
    grid = (regions // 4, 2, 2)
    pairs = []
    for dst in range(regions):
        spot = region_of(dst)
        src = tuple(spot[a] + sign * direction[a] for a in range(3))
        if all(0 <= src[a] < grid[a] for a in range(3)):
            pairs.append((4 * src[0] + 2 * src[1] + src[2], dst))
    return pairs


def exchange(piece, regions, direction, sign):
    pairs = neighbour_pairs(regions, direction, sign)
    if not pairs:
        return jnp.zeros_like(piece)
    return lax.ppermute(piece, "brick", pairs)


def halo_exchange(masked_piece, cot_piece, regions, direction):
    down = neighbour_pairs(regions, direction, 1)
    up = neighbour_pairs(regions, direction, -1)
    both = down + up
    sources = [a for a, _ in both]
    targets = [b for _, b in both]
    if not both or len(set(sources)) < len(both) or len(set(targets)) < len(both):
        return (
            exchange(masked_piece, regions, direction, 1),
            exchange(cot_piece, regions, direction, -1),
        )
    rank = lax.axis_index("brick")
    from_above = jnp.asarray([r in {b for _, b in down} for r in range(regions)])[rank]
    from_below = jnp.asarray([r in {b for _, b in up} for r in range(regions)])[rank]
    cut = masked_piece.size
    packed = jnp.concatenate([masked_piece.reshape(-1), cot_piece.reshape(-1)])
    got = lax.ppermute(packed, "brick", both)
    zero = jnp.zeros((), got.dtype)
    return (
        jnp.where(from_above, got[:cut], zero).reshape(masked_piece.shape),
        jnp.where(from_below, got[cut:], zero).reshape(cot_piece.shape),
    )


def forward_weight(up_weight):
    channels = up_weight.shape[1:]
    taps = jnp.pad(up_weight.reshape((3, 3, 3) + channels), ((0, 1), (0, 1), (0, 1), (0, 0), (0, 0)))
    for axis in range(3):
        taps = jnp.roll(taps, -1, axis=axis)
    return taps.reshape((2, 2, 2, 2, 2, 2) + channels)


def all_reduce(grads):
    devices = lax.axis_size("brick") * lax.axis_size("chip")
    lanes = grads.shape[-1]
    rows = grads.reshape(-1, lanes)
    size = rows.shape[0]
    chunk = -(-size // (2 * devices * 8)) * 8
    rows = jnp.pad(rows, ((0, 2 * chunk * devices - size), (0, 0)))
    rows = rows.reshape(2, devices, chunk, lanes)
    core = lax.axis_index("core")
    got = lax.ppermute(
        lax.dynamic_index_in_dim(rows, 1 - core, keepdims=False), "core", [(0, 1), (1, 0)]
    )
    half = lax.dynamic_index_in_dim(rows, core, keepdims=False) + got
    parts = lax.all_to_all(half, OTHERS, 0, 0, tiled=True)
    return parts.sum(axis=0), (devices, chunk, size)


def all_spread(reduced, plan, riders):
    devices, chunk, size = plan
    spread = jnp.broadcast_to(reduced[None], (devices,) + reduced.shape)
    half = lax.all_to_all(spread, OTHERS, 0, 0, tiled=True)
    half, riders = lax.optimization_barrier((half, riders))
    other = lax.ppermute(half, "core", [(0, 1), (1, 0)])
    core = lax.axis_index("core")
    whole = jnp.where(
        core == 0, jnp.concatenate([half, other]), jnp.concatenate([other, half])
    )
    return whole.reshape(-1, reduced.shape[-1])[:size], riders


def body(coarse, coarse_mask, skip, fine_mask, up_weight, fine_grad):
    regions = lax.axis_size("brick")
    size_x, size_y, merged = coarse.shape[2:]
    channels_out = up_weight.shape[1]
    channels_in = up_weight.shape[2]
    size_z = merged // channels_in
    fine_x, fine_y, fine_merged = skip.shape[2:]
    fine_z = fine_merged // channels_out
    counts = (size_x, size_y, size_z)

    coarse_keep = coarse_mask.reshape(size_x, size_y, size_z, 1).astype(jnp.bfloat16)
    masked = coarse.reshape(size_x, size_y, size_z, channels_in) * coarse_keep
    fine_keep = fine_mask.reshape(fine_x, fine_y, fine_z, 1)
    cotangent = fine_grad.reshape(fine_x, fine_y, fine_z, channels_out) * fine_keep.astype(
        jnp.bfloat16
    )

    halos = {}
    for direction in DIRECTIONS:
        masked_piece = masked[tuple(slice(0, 1) if flag else slice(None) for flag in direction)]
        cot_piece = cotangent[tuple(slice(-1, None) if flag else slice(None) for flag in direction)]
        halos[direction] = halo_exchange(masked_piece, cot_piece, regions, direction)
    widened = jnp.pad(cotangent, ((1, 1), (1, 1), (1, 1), (0, 0)))
    for direction in DIRECTIONS:
        target = tuple(
            slice(0, 1) if flag else slice(1, 1 + cotangent.shape[a])
            for a, flag in enumerate(direction)
        )
        widened = widened.at[target].set(halos[direction][1])
    paired = widened.reshape(size_x + 1, 2, size_y + 1, 2, size_z + 1, 2, channels_out)
    windows = []
    for kx in range(3):
        for ky in range(3):
            for kz in range(3):
                index = []
                for k, count in zip((kx, ky, kz), counts):
                    start = 1 if k == 2 else 0
                    index += [slice(start, start + count), 0 if k != 1 else 1]
                windows.append(paired[tuple(index)])
    gathered = jnp.stack(windows)
    grads = jnp.einsum(
        "kabco,abci->koi", gathered, masked, preferred_element_type=jnp.float32
    )
    grads, masked_late, weight_late = lax.optimization_barrier((grads, masked, up_weight))
    reduced, plan = all_reduce(grads)

    back = jnp.einsum(
        "kabco,koi->abci", gathered, up_weight, preferred_element_type=jnp.float32
    )
    coarse_grad = (
        (back * coarse_keep.astype(jnp.float32)).astype(jnp.bfloat16).reshape(coarse.shape)
    )

    extended = jnp.pad(masked_late, ((0, 1), (0, 1), (0, 1), (0, 0)))
    for direction in DIRECTIONS:
        target = tuple(
            slice(counts[a], counts[a] + 1) if flag else slice(0, counts[a])
            for a, flag in enumerate(direction)
        )
        extended = extended.at[target].set(halos[direction][0])

    shifted = jnp.stack(
        [
            extended[dx : dx + size_x, dy : dy + size_y, dz : dz + size_z]
            for dx, dy, dz in OFFSETS
        ]
    ).reshape((2, 2, 2, size_x, size_y, size_z, channels_in))
    parities = jnp.einsum(
        "xyzabci,xpyqzroi->apbqcro",
        shifted,
        forward_weight(weight_late),
        preferred_element_type=jnp.float32,
    )
    up = parities.reshape(fine_x, fine_y, fine_z, channels_out)
    fine = fine_keep.astype(jnp.float32) * (
        skip.reshape(fine_x, fine_y, fine_z, channels_out).astype(jnp.float32) + up
    )
    fine_out = fine.astype(jnp.bfloat16).reshape(skip.shape)

    scale = 1.0 / math.sqrt(regions * lax.axis_size("chip") * lax.axis_size("core") * size_x * size_y * size_z)
    weight_grad, (fine_out, coarse_grad) = all_spread(
        reduced * scale, plan, (fine_out, coarse_grad)
    )
    return (fine_out, coarse_grad, weight_grad.reshape(grads.shape))


def solution(mesh):
    brick, batch = mesh.shape["brick"], mesh.shape["batch"]
    pairs = Mesh(
        mesh.devices.reshape(brick, batch // 2, 2), ("brick", "chip", "core")
    )
    in_specs = (
        P(BATCH, "brick", None, None, None),
        P(BATCH, "brick", None),
        P(BATCH, "brick", None, None, None),
        P(BATCH, "brick", None),
        P(),
        P(BATCH, "brick", None, None, None),
    )
    out_specs = (P(BATCH, "brick", None, None, None), P(BATCH, "brick", None, None, None), P())
    return jax.shard_map(body, mesh=pairs, in_specs=in_specs, out_specs=out_specs, check_vma=False)
```

```python
import math

import jax
import jax.numpy as jnp
from jax import lax
from jax.sharding import Mesh, PartitionSpec as P

OFFSETS = tuple((dx, dy, dz) for dx in range(2) for dy in range(2) for dz in range(2))
DIRECTIONS = OFFSETS[1:]
BATCH = ("chip", "core")
OTHERS = ("brick", "chip")


def region_of(rank):
    return (rank // 4, rank // 2 % 2, rank % 2)


def neighbour_pairs(regions, direction, sign):
    grid = (regions // 4, 2, 2)
    pairs = []
    for dst in range(regions):
        spot = region_of(dst)
        src = tuple(spot[a] + sign * direction[a] for a in range(3))
        if all(0 <= src[a] < grid[a] for a in range(3)):
            pairs.append((4 * src[0] + 2 * src[1] + src[2], dst))
    return pairs


def exchange(piece, regions, direction, sign):
    pairs = neighbour_pairs(regions, direction, sign)
    if not pairs:
        return jnp.zeros_like(piece)
    return lax.ppermute(piece, "brick", pairs)


def halo_exchange(masked_piece, cot_piece, regions, direction):
    down = neighbour_pairs(regions, direction, 1)
    up = neighbour_pairs(regions, direction, -1)
    both = down + up
    sources = [a for a, _ in both]
    targets = [b for _, b in both]
    if not both or len(set(sources)) < len(both) or len(set(targets)) < len(both):
        return (
            exchange(masked_piece, regions, direction, 1),
            exchange(cot_piece, regions, direction, -1),
        )
    spot = region_of(lax.axis_index("brick"))
    grid = (regions // 4, 2, 2)
    sends_down = jnp.bool_(True)
    sends_up = jnp.bool_(True)
    for a in range(3):
        if direction[a]:
            sends_down = sends_down & (spot[a] >= 1)
            sends_up = sends_up & (spot[a] + 1 < grid[a])
    cut = masked_piece.size
    zero = jnp.zeros((), masked_piece.dtype)
    packed = jnp.concatenate(
        [
            jnp.where(sends_down, masked_piece.reshape(-1), zero),
            jnp.where(sends_up, cot_piece.reshape(-1), zero),
        ]
    )
    got = lax.ppermute(packed, "brick", both)
    return (got[:cut].reshape(masked_piece.shape), got[cut:].reshape(cot_piece.shape))


def forward_weight(up_weight):
    channels = up_weight.shape[1:]
    taps = jnp.pad(up_weight.reshape((3, 3, 3) + channels), ((0, 1), (0, 1), (0, 1), (0, 0), (0, 0)))
    for axis in range(3):
        taps = jnp.roll(taps, -1, axis=axis)
    return taps.reshape((2, 2, 2, 2, 2, 2) + channels)


def all_reduce(grads):
    devices = lax.axis_size("brick") * lax.axis_size("chip")
    lanes = grads.shape[-1]
    rows = grads.reshape(-1, lanes)
    size = rows.shape[0]
    chunk = -(-size // (2 * devices * 8)) * 8
    rows = jnp.pad(rows, ((0, 2 * chunk * devices - size), (0, 0)))
    rows = rows.reshape(2, devices, chunk, lanes)
    core = lax.axis_index("core")
    got = lax.ppermute(
        lax.dynamic_index_in_dim(rows, 1 - core, keepdims=False), "core", [(0, 1), (1, 0)]
    )
    half = lax.dynamic_index_in_dim(rows, core, keepdims=False) + got
    parts = lax.all_to_all(half, OTHERS, 0, 0, tiled=True)
    return parts.sum(axis=0), (devices, chunk, size)


def all_spread(reduced, plan, riders):
    devices, chunk, size = plan
    spread = jnp.broadcast_to(reduced[None], (devices,) + reduced.shape)
    half = lax.all_to_all(spread, OTHERS, 0, 0, tiled=True)
    half, riders = lax.optimization_barrier((half, riders))
    other = lax.ppermute(half, "core", [(0, 1), (1, 0)])
    lanes = reduced.shape[-1]
    rows = half.size // lanes
    three = jnp.concatenate([half, other, half]).reshape(-1, lanes)
    whole = lax.dynamic_slice_in_dim(three, lax.axis_index("core") * rows, size)
    return whole, riders


def body(coarse, coarse_mask, skip, fine_mask, up_weight, fine_grad):
    regions = lax.axis_size("brick")
    size_x, size_y, merged = coarse.shape[2:]
    channels_out = up_weight.shape[1]
    channels_in = up_weight.shape[2]
    size_z = merged // channels_in
    fine_x, fine_y, fine_merged = skip.shape[2:]
    fine_z = fine_merged // channels_out
    counts = (size_x, size_y, size_z)

    coarse_keep = coarse_mask.reshape(size_x, size_y, size_z, 1).astype(jnp.bfloat16)
    masked = coarse.reshape(size_x, size_y, size_z, channels_in) * coarse_keep
    fine_keep = fine_mask.reshape(fine_x, fine_y, fine_z, 1)
    cotangent = fine_grad.reshape(fine_x, fine_y, fine_z, channels_out) * fine_keep.astype(
        jnp.bfloat16
    )

    halos = {}
    for direction in DIRECTIONS:
        masked_piece = masked[tuple(slice(0, 1) if flag else slice(None) for flag in direction)]
        cot_piece = cotangent[tuple(slice(-1, None) if flag else slice(None) for flag in direction)]
        halos[direction] = halo_exchange(masked_piece, cot_piece, regions, direction)
    widened = jnp.pad(cotangent, ((1, 1), (1, 1), (1, 1), (0, 0)))
    for direction in DIRECTIONS:
        target = tuple(
            slice(0, 1) if flag else slice(1, 1 + cotangent.shape[a])
            for a, flag in enumerate(direction)
        )
        widened = widened.at[target].set(halos[direction][1])
    paired = widened.reshape(size_x + 1, 2, size_y + 1, 2, size_z + 1, 2, channels_out)
    windows = []
    for kx in range(3):
        for ky in range(3):
            for kz in range(3):
                index = []
                for k, count in zip((kx, ky, kz), counts):
                    start = 1 if k == 2 else 0
                    index += [slice(start, start + count), 0 if k != 1 else 1]
                windows.append(paired[tuple(index)])
    gathered = jnp.stack(windows)
    grads = jnp.einsum(
        "kabco,abci->koi", gathered, masked, preferred_element_type=jnp.float32
    )
    grads, masked_late, weight_late, skip, fine_keep = lax.optimization_barrier(
        (grads, masked, up_weight, skip, fine_keep)
    )
    reduced, plan = all_reduce(grads)

    back = jnp.einsum(
        "kabco,koi->abci", gathered, up_weight, preferred_element_type=jnp.float32
    )
    coarse_grad = (
        (back * coarse_keep.astype(jnp.float32)).astype(jnp.bfloat16).reshape(coarse.shape)
    )

    extended = jnp.pad(masked_late, ((0, 1), (0, 1), (0, 1), (0, 0)))
    for direction in DIRECTIONS:
        target = tuple(
            slice(counts[a], counts[a] + 1) if flag else slice(0, counts[a])
            for a, flag in enumerate(direction)
        )
        extended = extended.at[target].set(halos[direction][0])

    shifted = jnp.stack(
        [
            extended[dx : dx + size_x, dy : dy + size_y, dz : dz + size_z]
            for dx, dy, dz in OFFSETS
        ]
    ).reshape((2, 2, 2, size_x, size_y, size_z, channels_in))
    parities = jnp.einsum(
        "xyzabci,xpyqzroi->apbqcro",
        shifted,
        forward_weight(weight_late),
        preferred_element_type=jnp.float32,
    )
    up = parities.reshape(fine_x, fine_y, fine_z, channels_out)
    fine = fine_keep.astype(jnp.float32) * (
        skip.reshape(fine_x, fine_y, fine_z, channels_out).astype(jnp.float32) + up
    )
    fine_out = fine.astype(jnp.bfloat16).reshape(skip.shape)

    scale = 1.0 / math.sqrt(regions * lax.axis_size("chip") * lax.axis_size("core") * size_x * size_y * size_z)
    weight_grad, (fine_out, coarse_grad) = all_spread(
        reduced * scale, plan, (fine_out, coarse_grad)
    )
    return (fine_out, coarse_grad, weight_grad.reshape(grads.shape))


def solution(mesh):
    brick, batch = mesh.shape["brick"], mesh.shape["batch"]
    pairs = Mesh(
        mesh.devices.reshape(brick, batch // 2, 2), ("brick", "chip", "core")
    )
    in_specs = (
        P(BATCH, "brick", None, None, None),
        P(BATCH, "brick", None),
        P(BATCH, "brick", None, None, None),
        P(BATCH, "brick", None),
        P(),
        P(BATCH, "brick", None, None, None),
    )
    out_specs = (P(BATCH, "brick", None, None, None), P(BATCH, "brick", None, None, None), P())
    return jax.shard_map(body, mesh=pairs, in_specs=in_specs, out_specs=out_specs, check_vma=False)
```

```python
import math

import jax
import jax.numpy as jnp
from jax import lax
from jax.sharding import Mesh, PartitionSpec as P

OFFSETS = tuple((dx, dy, dz) for dx in range(2) for dy in range(2) for dz in range(2))
DIRECTIONS = OFFSETS[1:]
BATCH = ("chip", "core")
OTHERS = ("brick", "chip")


def region_of(rank):
    return (rank // 4, rank // 2 % 2, rank % 2)


def neighbour_pairs(regions, direction, sign):
    grid = (regions // 4, 2, 2)
    pairs = []
    for dst in range(regions):
        spot = region_of(dst)
        src = tuple(spot[a] + sign * direction[a] for a in range(3))
        if all(0 <= src[a] < grid[a] for a in range(3)):
            pairs.append((4 * src[0] + 2 * src[1] + src[2], dst))
    return pairs


def exchange(piece, regions, direction, sign):
    pairs = neighbour_pairs(regions, direction, sign)
    if not pairs:
        return jnp.zeros_like(piece)
    return lax.ppermute(piece, "brick", pairs)


def halo_exchange(masked_piece, cot_piece, regions, direction):
    down = neighbour_pairs(regions, direction, 1)
    up = neighbour_pairs(regions, direction, -1)
    both = down + up
    sources = [a for a, _ in both]
    targets = [b for _, b in both]
    if not both or len(set(sources)) < len(both) or len(set(targets)) < len(both):
        return (
            exchange(masked_piece, regions, direction, 1),
            exchange(cot_piece, regions, direction, -1),
        )
    spot = region_of(lax.axis_index("brick"))
    grid = (regions // 4, 2, 2)
    sends_down = jnp.bool_(True)
    sends_up = jnp.bool_(True)
    for a in range(3):
        if direction[a]:
            sends_down = sends_down & (spot[a] >= 1)
            sends_up = sends_up & (spot[a] + 1 < grid[a])
    cut = masked_piece.size
    zero = jnp.zeros((), masked_piece.dtype)
    packed = jnp.concatenate(
        [
            jnp.where(sends_down, masked_piece.reshape(-1), zero),
            jnp.where(sends_up, cot_piece.reshape(-1), zero),
        ]
    )
    got = lax.ppermute(packed, "brick", both)
    return (got[:cut].reshape(masked_piece.shape), got[cut:].reshape(cot_piece.shape))


def forward_weight(up_weight):
    channels = up_weight.shape[1:]
    taps = jnp.pad(up_weight.reshape((3, 3, 3) + channels), ((0, 1), (0, 1), (0, 1), (0, 0), (0, 0)))
    for axis in range(3):
        taps = jnp.roll(taps, -1, axis=axis)
    return taps.reshape((2, 2, 2, 2, 2, 2) + channels)


def all_reduce(grads):
    devices = lax.axis_size("brick") * lax.axis_size("chip")
    lanes = grads.shape[-1]
    rows = grads.reshape(-1, lanes)
    size = rows.shape[0]
    chunk = -(-size // (2 * devices * 8)) * 8
    rows = jnp.pad(rows, ((0, 2 * chunk * devices - size), (0, 0)))
    rows = rows.reshape(2, devices, chunk, lanes)
    core = lax.axis_index("core")
    got = lax.ppermute(
        lax.dynamic_index_in_dim(rows, 1 - core, keepdims=False), "core", [(0, 1), (1, 0)]
    )
    half = lax.dynamic_index_in_dim(rows, core, keepdims=False) + got
    parts = lax.all_to_all(half, OTHERS, 0, 0, tiled=True)
    return parts.sum(axis=0), (devices, chunk, size)


def all_spread(reduced, plan, riders):
    devices, chunk, size = plan
    spread = jnp.broadcast_to(reduced[None], (devices,) + reduced.shape)
    half = lax.all_to_all(spread, OTHERS, 0, 0, tiled=True)
    half, riders = lax.optimization_barrier((half, riders))
    other = lax.ppermute(half, "core", [(0, 1), (1, 0)])
    lanes = reduced.shape[-1]
    rows = half.size // lanes
    three = jnp.concatenate([half, other, half]).reshape(-1, lanes)
    whole = lax.dynamic_slice_in_dim(three, lax.axis_index("core") * rows, size)
    return whole, riders


def body(coarse, coarse_mask, skip, fine_mask, up_weight, fine_grad):
    regions = lax.axis_size("brick")
    size_x, size_y, merged = coarse.shape[2:]
    channels_out = up_weight.shape[1]
    channels_in = up_weight.shape[2]
    size_z = merged // channels_in
    fine_x, fine_y, fine_merged = skip.shape[2:]
    fine_z = fine_merged // channels_out
    counts = (size_x, size_y, size_z)

    coarse_keep = coarse_mask.reshape(size_x, size_y, size_z, 1).astype(jnp.bfloat16)
    masked = coarse.reshape(size_x, size_y, size_z, channels_in) * coarse_keep
    fine_keep = fine_mask.reshape(fine_x, fine_y, fine_z, 1)
    cotangent = fine_grad.reshape(fine_x, fine_y, fine_z, channels_out) * fine_keep.astype(
        jnp.bfloat16
    )

    halos = {}
    for direction in DIRECTIONS:
        masked_piece = masked[tuple(slice(0, 1) if flag else slice(None) for flag in direction)]
        cot_piece = cotangent[tuple(slice(-1, None) if flag else slice(None) for flag in direction)]
        halos[direction] = halo_exchange(masked_piece, cot_piece, regions, direction)
    widened = jnp.pad(cotangent, ((1, 1), (1, 1), (1, 1), (0, 0)))
    for direction in DIRECTIONS:
        target = tuple(
            slice(0, 1) if flag else slice(1, 1 + cotangent.shape[a])
            for a, flag in enumerate(direction)
        )
        widened = widened.at[target].set(halos[direction][1])
    window = tuple(2 * c + 1 for c in counts)
    grads = lax.conv_general_dilated(
        widened[: window[0], : window[1], : window[2]].transpose(3, 0, 1, 2)[:, None],
        masked.transpose(3, 0, 1, 2)[:, None],
        (1, 1, 1),
        "VALID",
        rhs_dilation=(2, 2, 2),
        preferred_element_type=jnp.float32,
    )
    grads = grads.transpose(2, 3, 4, 0, 1).reshape(27, channels_out, channels_in)
    grads, masked_late, weight_late, skip, fine_keep, widened = lax.optimization_barrier(
        (grads, masked, up_weight, skip, fine_keep, widened)
    )
    paired = widened.reshape(size_x + 1, 2, size_y + 1, 2, size_z + 1, 2, channels_out)
    windows = []
    for kx in range(3):
        for ky in range(3):
            for kz in range(3):
                index = []
                for k, count in zip((kx, ky, kz), counts):
                    start = 1 if k == 2 else 0
                    index += [slice(start, start + count), 0 if k != 1 else 1]
                windows.append(paired[tuple(index)])
    gathered = jnp.stack(windows)
    reduced, plan = all_reduce(grads)

    back = jnp.einsum(
        "kabco,koi->abci", gathered, up_weight, preferred_element_type=jnp.float32
    )
    coarse_grad = (
        (back * coarse_keep.astype(jnp.float32)).astype(jnp.bfloat16).reshape(coarse.shape)
    )

    extended = jnp.pad(masked_late, ((0, 1), (0, 1), (0, 1), (0, 0)))
    for direction in DIRECTIONS:
        target = tuple(
            slice(counts[a], counts[a] + 1) if flag else slice(0, counts[a])
            for a, flag in enumerate(direction)
        )
        extended = extended.at[target].set(halos[direction][0])

    shifted = jnp.stack(
        [
            extended[dx : dx + size_x, dy : dy + size_y, dz : dz + size_z]
            for dx, dy, dz in OFFSETS
        ]
    ).reshape((2, 2, 2, size_x, size_y, size_z, channels_in))
    parities = jnp.einsum(
        "xyzabci,xpyqzroi->apbqcro",
        shifted,
        forward_weight(weight_late),
        preferred_element_type=jnp.float32,
    )
    up = parities.reshape(fine_x, fine_y, fine_z, channels_out)
    fine = fine_keep.astype(jnp.float32) * (
        skip.reshape(fine_x, fine_y, fine_z, channels_out).astype(jnp.float32) + up
    )
    fine_out = fine.astype(jnp.bfloat16).reshape(skip.shape)

    scale = 1.0 / math.sqrt(regions * lax.axis_size("chip") * lax.axis_size("core") * size_x * size_y * size_z)
    weight_grad, (fine_out, coarse_grad) = all_spread(
        reduced * scale, plan, (fine_out, coarse_grad)
    )
    return (fine_out, coarse_grad, weight_grad.reshape(grads.shape))


def solution(mesh):
    brick, batch = mesh.shape["brick"], mesh.shape["batch"]
    pairs = Mesh(
        mesh.devices.reshape(brick, batch // 2, 2), ("brick", "chip", "core")
    )
    in_specs = (
        P(BATCH, "brick", None, None, None),
        P(BATCH, "brick", None),
        P(BATCH, "brick", None, None, None),
        P(BATCH, "brick", None),
        P(),
        P(BATCH, "brick", None, None, None),
    )
    out_specs = (P(BATCH, "brick", None, None, None), P(BATCH, "brick", None, None, None), P())
    return jax.shard_map(body, mesh=pairs, in_specs=in_specs, out_specs=out_specs, check_vma=False)
```

```python
import math

import jax
import jax.numpy as jnp
from jax import lax
from jax.sharding import Mesh, PartitionSpec as P

OFFSETS = tuple((dx, dy, dz) for dx in range(2) for dy in range(2) for dz in range(2))
DIRECTIONS = OFFSETS[1:]
BATCH = ("chip", "core")
OTHERS = ("brick", "chip")


def region_of(rank):
    return (rank // 4, rank // 2 % 2, rank % 2)


def neighbour_pairs(regions, direction, sign):
    grid = (regions // 4, 2, 2)
    pairs = []
    for dst in range(regions):
        spot = region_of(dst)
        src = tuple(spot[a] + sign * direction[a] for a in range(3))
        if all(0 <= src[a] < grid[a] for a in range(3)):
            pairs.append((4 * src[0] + 2 * src[1] + src[2], dst))
    return pairs


def exchange(piece, regions, direction, sign):
    pairs = neighbour_pairs(regions, direction, sign)
    if not pairs:
        return jnp.zeros_like(piece)
    return lax.ppermute(piece, "brick", pairs)


def halo_exchange(masked_piece, cot_piece, regions, direction):
    down = neighbour_pairs(regions, direction, 1)
    up = neighbour_pairs(regions, direction, -1)
    both = down + up
    sources = [a for a, _ in both]
    targets = [b for _, b in both]
    if not both or len(set(sources)) < len(both) or len(set(targets)) < len(both):
        return (
            exchange(masked_piece, regions, direction, 1),
            exchange(cot_piece, regions, direction, -1),
        )
    spot = region_of(lax.axis_index("brick"))
    grid = (regions // 4, 2, 2)
    sends_down = jnp.bool_(True)
    sends_up = jnp.bool_(True)
    for a in range(3):
        if direction[a]:
            sends_down = sends_down & (spot[a] >= 1)
            sends_up = sends_up & (spot[a] + 1 < grid[a])
    cut = masked_piece.size
    zero = jnp.zeros((), masked_piece.dtype)
    packed = jnp.concatenate(
        [
            jnp.where(sends_down, masked_piece.reshape(-1), zero),
            jnp.where(sends_up, cot_piece.reshape(-1), zero),
        ]
    )
    got = lax.ppermute(packed, "brick", both)
    return (got[:cut].reshape(masked_piece.shape), got[cut:].reshape(cot_piece.shape))


def forward_weight(up_weight):
    channels = up_weight.shape[1:]
    taps = jnp.pad(up_weight.reshape((3, 3, 3) + channels), ((0, 1), (0, 1), (0, 1), (0, 0), (0, 0)))
    for axis in range(3):
        taps = jnp.roll(taps, -1, axis=axis)
    return taps.reshape((2, 2, 2, 2, 2, 2) + channels)


def all_reduce(grads):
    devices = lax.axis_size("brick") * lax.axis_size("chip")
    lanes = grads.shape[-1]
    rows = grads.reshape(-1, lanes)
    size = rows.shape[0]
    chunk = -(-size // (2 * devices * 8)) * 8
    rows = jnp.pad(rows, ((0, 2 * chunk * devices - size), (0, 0)))
    rows = rows.reshape(2, devices, chunk, lanes)
    core = lax.axis_index("core")
    got = lax.ppermute(
        lax.dynamic_index_in_dim(rows, 1 - core, keepdims=False), "core", [(0, 1), (1, 0)]
    )
    half = lax.dynamic_index_in_dim(rows, core, keepdims=False) + got
    parts = lax.all_to_all(half, OTHERS, 0, 0, tiled=True)
    return parts.sum(axis=0), (devices, chunk, size)


def all_spread(reduced, plan, riders):
    devices, chunk, size = plan
    spread = jnp.broadcast_to(reduced[None], (devices,) + reduced.shape)
    half = lax.all_to_all(spread, OTHERS, 0, 0, tiled=True)
    half, riders = lax.optimization_barrier((half, riders))
    other = lax.ppermute(half, "core", [(0, 1), (1, 0)])
    lanes = reduced.shape[-1]
    rows = half.size // lanes
    three = jnp.concatenate([half, other, half]).reshape(-1, lanes)
    whole = lax.dynamic_slice_in_dim(three, lax.axis_index("core") * rows, size)
    return whole, riders


def body(coarse, coarse_mask, skip, fine_mask, up_weight, fine_grad):
    regions = lax.axis_size("brick")
    size_x, size_y, merged = coarse.shape[2:]
    channels_out = up_weight.shape[1]
    channels_in = up_weight.shape[2]
    size_z = merged // channels_in
    fine_x, fine_y, fine_merged = skip.shape[2:]
    fine_z = fine_merged // channels_out
    counts = (size_x, size_y, size_z)

    coarse_keep = coarse_mask.reshape(size_x, size_y, size_z, 1).astype(jnp.bfloat16)
    masked = coarse.reshape(size_x, size_y, size_z, channels_in) * coarse_keep
    fine_keep = fine_mask.reshape(fine_x, fine_y, fine_z, 1)
    cotangent = fine_grad.reshape(fine_x, fine_y, fine_z, channels_out) * fine_keep.astype(
        jnp.bfloat16
    )

    halos = {}
    for direction in DIRECTIONS:
        masked_piece = masked[tuple(slice(0, 1) if flag else slice(None) for flag in direction)]
        cot_piece = cotangent[tuple(slice(-1, None) if flag else slice(None) for flag in direction)]
        halos[direction] = halo_exchange(masked_piece, cot_piece, regions, direction)
    widened = jnp.pad(cotangent, ((1, 1), (1, 1), (1, 1), (0, 0)))
    for direction in DIRECTIONS:
        target = tuple(
            slice(0, 1) if flag else slice(1, 1 + cotangent.shape[a])
            for a, flag in enumerate(direction)
        )
        widened = widened.at[target].set(halos[direction][1])
    window = tuple(2 * c + 1 for c in counts)
    grads = lax.conv_general_dilated(
        widened[: window[0], : window[1], : window[2]].transpose(3, 0, 1, 2)[:, None],
        masked.transpose(3, 0, 1, 2)[:, None],
        (1, 1, 1),
        "VALID",
        rhs_dilation=(2, 2, 2),
        preferred_element_type=jnp.float32,
    )
    grads = grads.transpose(2, 3, 4, 0, 1).reshape(27, channels_out, channels_in)
    grads, masked_late, weight_late, skip, fine_keep = lax.optimization_barrier(
        (grads, masked, up_weight, skip, fine_keep)
    )
    reduced, plan = all_reduce(grads)

    back = lax.conv_general_dilated(
        widened[None, : window[0], : window[1], : window[2]],
        up_weight.reshape((3, 3, 3, channels_out, channels_in)),
        (2, 2, 2),
        "VALID",
        dimension_numbers=("NXYZC", "XYZIO", "NXYZC"),
        preferred_element_type=jnp.float32,
    )[0]
    coarse_grad = (
        (back * coarse_keep.astype(jnp.float32)).astype(jnp.bfloat16).reshape(coarse.shape)
    )

    extended = jnp.pad(masked_late, ((0, 1), (0, 1), (0, 1), (0, 0)))
    for direction in DIRECTIONS:
        target = tuple(
            slice(counts[a], counts[a] + 1) if flag else slice(0, counts[a])
            for a, flag in enumerate(direction)
        )
        extended = extended.at[target].set(halos[direction][0])

    shifted = jnp.stack(
        [
            extended[dx : dx + size_x, dy : dy + size_y, dz : dz + size_z]
            for dx, dy, dz in OFFSETS
        ]
    ).reshape((2, 2, 2, size_x, size_y, size_z, channels_in))
    parities = jnp.einsum(
        "xyzabci,xpyqzroi->apbqcro",
        shifted,
        forward_weight(weight_late),
        preferred_element_type=jnp.float32,
    )
    up = parities.reshape(fine_x, fine_y, fine_z, channels_out)
    fine = fine_keep.astype(jnp.float32) * (
        skip.reshape(fine_x, fine_y, fine_z, channels_out).astype(jnp.float32) + up
    )
    fine_out = fine.astype(jnp.bfloat16).reshape(skip.shape)

    scale = 1.0 / math.sqrt(regions * lax.axis_size("chip") * lax.axis_size("core") * size_x * size_y * size_z)
    weight_grad, (fine_out, coarse_grad) = all_spread(
        reduced * scale, plan, (fine_out, coarse_grad)
    )
    return (fine_out, coarse_grad, weight_grad.reshape(grads.shape))


def solution(mesh):
    brick, batch = mesh.shape["brick"], mesh.shape["batch"]
    pairs = Mesh(
        mesh.devices.reshape(brick, batch // 2, 2), ("brick", "chip", "core")
    )
    in_specs = (
        P(BATCH, "brick", None, None, None),
        P(BATCH, "brick", None),
        P(BATCH, "brick", None, None, None),
        P(BATCH, "brick", None),
        P(),
        P(BATCH, "brick", None, None, None),
    )
    out_specs = (P(BATCH, "brick", None, None, None), P(BATCH, "brick", None, None, None), P())
    return jax.shard_map(body, mesh=pairs, in_specs=in_specs, out_specs=out_specs, check_vma=False)
```

```python
import math

import jax
import jax.numpy as jnp
from jax import lax
from jax.sharding import Mesh, PartitionSpec as P

OFFSETS = tuple((dx, dy, dz) for dx in range(2) for dy in range(2) for dz in range(2))
DIRECTIONS = OFFSETS[1:]
BATCH = ("chip", "core")
OTHERS = ("brick", "chip")


def region_of(rank):
    return (rank // 4, rank // 2 % 2, rank % 2)


def neighbour_pairs(regions, direction, sign):
    grid = (regions // 4, 2, 2)
    pairs = []
    for dst in range(regions):
        spot = region_of(dst)
        src = tuple(spot[a] + sign * direction[a] for a in range(3))
        if all(0 <= src[a] < grid[a] for a in range(3)):
            pairs.append((4 * src[0] + 2 * src[1] + src[2], dst))
    return pairs


def exchange(piece, regions, direction, sign):
    pairs = neighbour_pairs(regions, direction, sign)
    if not pairs:
        return jnp.zeros_like(piece)
    return lax.ppermute(piece, "brick", pairs)


def halo_exchange(masked_piece, cot_piece, regions, direction):
    down = neighbour_pairs(regions, direction, 1)
    up = neighbour_pairs(regions, direction, -1)
    both = down + up
    sources = [a for a, _ in both]
    targets = [b for _, b in both]
    if not both or len(set(sources)) < len(both) or len(set(targets)) < len(both):
        return (
            exchange(masked_piece, regions, direction, 1),
            exchange(cot_piece, regions, direction, -1),
        )
    spot = region_of(lax.axis_index("brick"))
    grid = (regions // 4, 2, 2)
    sends_down = jnp.bool_(True)
    sends_up = jnp.bool_(True)
    for a in range(3):
        if direction[a]:
            sends_down = sends_down & (spot[a] >= 1)
            sends_up = sends_up & (spot[a] + 1 < grid[a])
    cut = masked_piece.size
    zero = jnp.zeros((), masked_piece.dtype)
    packed = jnp.concatenate(
        [
            jnp.where(sends_down, masked_piece.reshape(-1), zero),
            jnp.where(sends_up, cot_piece.reshape(-1), zero),
        ]
    )
    got = lax.ppermute(packed, "brick", both)
    return (got[:cut].reshape(masked_piece.shape), got[cut:].reshape(cot_piece.shape))


def forward_weight(up_weight):
    channels = up_weight.shape[1:]
    taps = jnp.pad(up_weight.reshape((3, 3, 3) + channels), ((0, 1), (0, 1), (0, 1), (0, 0), (0, 0)))
    for axis in range(3):
        taps = jnp.roll(taps, -1, axis=axis)
    return taps.reshape((2, 2, 2, 2, 2, 2) + channels)


def all_reduce(half):
    devices = lax.axis_size("brick") * lax.axis_size("chip")
    lanes = half.shape[-1]
    rows = half.reshape(-1, lanes)
    size = rows.shape[0]
    chunk = -(-size // (devices * 8)) * 8
    rows = jnp.pad(rows, ((0, chunk * devices - size), (0, 0)))
    parts = lax.all_to_all(rows.reshape(devices, chunk, lanes), OTHERS, 0, 0, tiled=True)
    return parts.sum(axis=0), (devices, chunk, size, half.shape)


def all_spread(reduced, plan, riders):
    devices, chunk, size, shape = plan
    spread = jnp.broadcast_to(reduced[None], (devices,) + reduced.shape)
    half = lax.all_to_all(spread, OTHERS, 0, 0, tiled=True)
    half, riders = lax.optimization_barrier((half, riders))
    half = half.reshape(-1, reduced.shape[-1])[:size].reshape(shape)
    other = lax.ppermute(half, "core", [(0, 1), (1, 0)])
    three = jnp.stack([half, other, half], axis=1)
    whole = lax.dynamic_slice_in_dim(three, lax.axis_index("core"), 2, axis=1)
    return whole.reshape(shape[0], 2 * shape[1], shape[2]), riders


def body(coarse, coarse_mask, skip, fine_mask, up_weight, fine_grad):
    regions = lax.axis_size("brick")
    size_x, size_y, merged = coarse.shape[2:]
    channels_out = up_weight.shape[1]
    channels_in = up_weight.shape[2]
    size_z = merged // channels_in
    fine_x, fine_y, fine_merged = skip.shape[2:]
    fine_z = fine_merged // channels_out
    counts = (size_x, size_y, size_z)

    coarse_keep = coarse_mask.reshape(size_x, size_y, size_z, 1).astype(jnp.bfloat16)
    masked = coarse.reshape(size_x, size_y, size_z, channels_in) * coarse_keep
    fine_keep = fine_mask.reshape(fine_x, fine_y, fine_z, 1)
    cotangent = fine_grad.reshape(fine_x, fine_y, fine_z, channels_out) * fine_keep.astype(
        jnp.bfloat16
    )

    halos = {}
    for direction in DIRECTIONS:
        masked_piece = masked[tuple(slice(0, 1) if flag else slice(None) for flag in direction)]
        cot_piece = cotangent[tuple(slice(-1, None) if flag else slice(None) for flag in direction)]
        halos[direction] = halo_exchange(masked_piece, cot_piece, regions, direction)
    widened = jnp.pad(cotangent, ((1, 1), (1, 1), (1, 1), (0, 0)))
    for direction in DIRECTIONS:
        target = tuple(
            slice(0, 1) if flag else slice(1, 1 + cotangent.shape[a])
            for a, flag in enumerate(direction)
        )
        widened = widened.at[target].set(halos[direction][1])
    window = tuple(2 * c + 1 for c in counts)
    trimmed = widened[: window[0], : window[1], : window[2]]
    core = lax.axis_index("core")
    share = channels_out // 2
    mine = lax.dynamic_slice_in_dim(trimmed, core * share, share, axis=3)
    theirs = lax.dynamic_slice_in_dim(trimmed, (1 - core) * share, share, axis=3)
    cut = theirs.size
    got = lax.ppermute(
        jnp.concatenate([theirs.reshape(-1), masked.reshape(-1)]), "core", [(0, 1), (1, 0)]
    )
    grads = lax.conv_general_dilated(
        jnp.stack([mine, got[:cut].reshape(theirs.shape)], axis=-1),
        jnp.stack([masked, got[cut:].reshape(masked.shape)], axis=-1),
        (1, 1, 1),
        "VALID",
        rhs_dilation=(2, 2, 2),
        dimension_numbers=("XYZNC", "XYZOI", "XYZNC"),
        preferred_element_type=jnp.float32,
    ).reshape(27, share, channels_in)
    grads, masked_late, weight_late, skip, fine_keep = lax.optimization_barrier(
        (grads, masked, up_weight, skip, fine_keep)
    )
    reduced, plan = all_reduce(grads)

    back = lax.conv_general_dilated(
        widened[None, : window[0], : window[1], : window[2]],
        up_weight.reshape((3, 3, 3, channels_out, channels_in)),
        (2, 2, 2),
        "VALID",
        dimension_numbers=("NXYZC", "XYZIO", "NXYZC"),
        preferred_element_type=jnp.float32,
    )[0]
    coarse_grad = (
        (back * coarse_keep.astype(jnp.float32)).astype(jnp.bfloat16).reshape(coarse.shape)
    )

    extended = jnp.pad(masked_late, ((0, 1), (0, 1), (0, 1), (0, 0)))
    for direction in DIRECTIONS:
        target = tuple(
            slice(counts[a], counts[a] + 1) if flag else slice(0, counts[a])
            for a, flag in enumerate(direction)
        )
        extended = extended.at[target].set(halos[direction][0])

    shifted = jnp.stack(
        [
            extended[dx : dx + size_x, dy : dy + size_y, dz : dz + size_z]
            for dx, dy, dz in OFFSETS
        ]
    ).reshape((2, 2, 2, size_x, size_y, size_z, channels_in))
    parities = jnp.einsum(
        "xyzabci,xpyqzroi->apbqcro",
        shifted,
        forward_weight(weight_late),
        preferred_element_type=jnp.float32,
    )
    up = parities.reshape(fine_x, fine_y, fine_z, channels_out)
    fine = fine_keep.astype(jnp.float32) * (
        skip.reshape(fine_x, fine_y, fine_z, channels_out).astype(jnp.float32) + up
    )
    fine_out = fine.astype(jnp.bfloat16).reshape(skip.shape)

    scale = 1.0 / math.sqrt(regions * lax.axis_size("chip") * lax.axis_size("core") * size_x * size_y * size_z)
    weight_grad, (fine_out, coarse_grad) = all_spread(
        reduced * scale, plan, (fine_out, coarse_grad)
    )
    return (fine_out, coarse_grad, weight_grad)


def solution(mesh):
    brick, batch = mesh.shape["brick"], mesh.shape["batch"]
    pairs = Mesh(
        mesh.devices.reshape(brick, batch // 2, 2), ("brick", "chip", "core")
    )
    in_specs = (
        P(BATCH, "brick", None, None, None),
        P(BATCH, "brick", None),
        P(BATCH, "brick", None, None, None),
        P(BATCH, "brick", None),
        P(),
        P(BATCH, "brick", None, None, None),
    )
    out_specs = (P(BATCH, "brick", None, None, None), P(BATCH, "brick", None, None, None), P())
    return jax.shard_map(body, mesh=pairs, in_specs=in_specs, out_specs=out_specs, check_vma=False)
```

```python
import math

import jax
import jax.numpy as jnp
from jax import lax
from jax.sharding import Mesh, PartitionSpec as P

OFFSETS = tuple((dx, dy, dz) for dx in range(2) for dy in range(2) for dz in range(2))
DIRECTIONS = OFFSETS[1:]
BATCH = ("chip", "core")
OTHERS = ("brick", "chip")


def region_of(rank):
    return (rank // 4, rank // 2 % 2, rank % 2)


def neighbour_pairs(regions, direction, sign):
    grid = (regions // 4, 2, 2)
    pairs = []
    for dst in range(regions):
        spot = region_of(dst)
        src = tuple(spot[a] + sign * direction[a] for a in range(3))
        if all(0 <= src[a] < grid[a] for a in range(3)):
            pairs.append((4 * src[0] + 2 * src[1] + src[2], dst))
    return pairs


def exchange(piece, regions, direction, sign):
    pairs = neighbour_pairs(regions, direction, sign)
    if not pairs:
        return jnp.zeros_like(piece)
    return lax.ppermute(piece, "brick", pairs)


def halo_exchange(masked_piece, cot_piece, regions, direction):
    down = neighbour_pairs(regions, direction, 1)
    up = neighbour_pairs(regions, direction, -1)
    both = down + up
    sources = [a for a, _ in both]
    targets = [b for _, b in both]
    if not both or len(set(sources)) < len(both) or len(set(targets)) < len(both):
        return (
            exchange(masked_piece, regions, direction, 1),
            exchange(cot_piece, regions, direction, -1),
        )
    spot = region_of(lax.axis_index("brick"))
    grid = (regions // 4, 2, 2)
    sends_down = jnp.bool_(True)
    sends_up = jnp.bool_(True)
    for a in range(3):
        if direction[a]:
            sends_down = sends_down & (spot[a] >= 1)
            sends_up = sends_up & (spot[a] + 1 < grid[a])
    cut = masked_piece.size
    zero = jnp.zeros((), masked_piece.dtype)
    packed = jnp.concatenate(
        [
            jnp.where(sends_down, masked_piece.reshape(-1), zero),
            jnp.where(sends_up, cot_piece.reshape(-1), zero),
        ]
    )
    got = lax.ppermute(packed, "brick", both)
    return (got[:cut].reshape(masked_piece.shape), got[cut:].reshape(cot_piece.shape))


def forward_weight(up_weight):
    channels = up_weight.shape[1:]
    taps = jnp.pad(up_weight.reshape((3, 3, 3) + channels), ((0, 1), (0, 1), (0, 1), (0, 0), (0, 0)))
    for axis in range(3):
        taps = jnp.roll(taps, -1, axis=axis)
    return taps.reshape((2, 2, 2, 2, 2, 2) + channels)


def all_reduce(half):
    devices = lax.axis_size("brick") * lax.axis_size("chip")
    lanes = half.shape[-1]
    rows = half.reshape(-1, lanes)
    size = rows.shape[0]
    chunk = -(-size // (devices * 8)) * 8
    rows = jnp.pad(rows, ((0, chunk * devices - size), (0, 0)))
    parts = lax.all_to_all(rows.reshape(devices, chunk, lanes), OTHERS, 0, 0, tiled=True)
    return parts.sum(axis=0), (devices, chunk, size, half.shape)


def all_spread(reduced, plan, riders):
    devices, chunk, size, shape = plan
    spread = jnp.broadcast_to(reduced[None], (devices,) + reduced.shape)
    half = lax.all_to_all(spread, OTHERS, 0, 0, tiled=True)
    half, riders = lax.optimization_barrier((half, riders))
    half = half.reshape(-1, reduced.shape[-1])[:size].reshape(shape)
    other = lax.ppermute(half, "core", [(0, 1), (1, 0)])
    three = jnp.stack([half, other, half], axis=1)
    whole = lax.dynamic_slice_in_dim(three, lax.axis_index("core"), 2, axis=1)
    return whole.reshape(shape[0], 2 * shape[1], shape[2]), riders


def body(coarse, coarse_mask, skip, fine_mask, up_weight, fine_grad):
    regions = lax.axis_size("brick")
    size_x, size_y, merged = coarse.shape[2:]
    channels_out = up_weight.shape[1]
    channels_in = up_weight.shape[2]
    size_z = merged // channels_in
    fine_x, fine_y, fine_merged = skip.shape[2:]
    fine_z = fine_merged // channels_out
    counts = (size_x, size_y, size_z)

    coarse_keep = coarse_mask.reshape(size_x, size_y, size_z, 1).astype(jnp.bfloat16)
    masked = coarse.reshape(size_x, size_y, size_z, channels_in) * coarse_keep
    fine_keep = fine_mask.reshape(fine_x, fine_y, fine_z, 1)
    cotangent = fine_grad.reshape(fine_x, fine_y, fine_z, channels_out) * fine_keep.astype(
        jnp.bfloat16
    )

    halos = {}
    for direction in DIRECTIONS:
        masked_piece = masked[tuple(slice(0, 1) if flag else slice(None) for flag in direction)]
        cot_piece = cotangent[tuple(slice(-1, None) if flag else slice(None) for flag in direction)]
        halos[direction] = halo_exchange(masked_piece, cot_piece, regions, direction)
    widened = jnp.pad(cotangent, ((1, 1), (1, 1), (1, 1), (0, 0)))
    for direction in DIRECTIONS:
        target = tuple(
            slice(0, 1) if flag else slice(1, 1 + cotangent.shape[a])
            for a, flag in enumerate(direction)
        )
        widened = widened.at[target].set(halos[direction][1])
    window = tuple(2 * c + 1 for c in counts)
    trimmed = widened[: window[0], : window[1], : window[2]]
    core = lax.axis_index("core")
    share = channels_out // 2

    def channel_grads(start):
        part = lax.dynamic_slice_in_dim(trimmed, start, share, axis=3)
        return lax.conv_general_dilated(
            part[..., None],
            masked[..., None],
            (1, 1, 1),
            "VALID",
            rhs_dilation=(2, 2, 2),
            dimension_numbers=("XYZNC", "XYZOI", "XYZNC"),
            preferred_element_type=jnp.float32,
        ).reshape(27, share, channels_in)

    got = lax.ppermute(channel_grads((1 - core) * share), "core", [(0, 1), (1, 0)])
    grads = channel_grads(core * share) + got
    grads, masked_late, weight_late, skip, fine_keep = lax.optimization_barrier(
        (grads, masked, up_weight, skip, fine_keep)
    )
    reduced, plan = all_reduce(grads)

    back = lax.conv_general_dilated(
        widened[None, : window[0], : window[1], : window[2]],
        up_weight.reshape((3, 3, 3, channels_out, channels_in)),
        (2, 2, 2),
        "VALID",
        dimension_numbers=("NXYZC", "XYZIO", "NXYZC"),
        preferred_element_type=jnp.float32,
    )[0]
    coarse_grad = (
        (back * coarse_keep.astype(jnp.float32)).astype(jnp.bfloat16).reshape(coarse.shape)
    )

    extended = jnp.pad(masked_late, ((0, 1), (0, 1), (0, 1), (0, 0)))
    for direction in DIRECTIONS:
        target = tuple(
            slice(counts[a], counts[a] + 1) if flag else slice(0, counts[a])
            for a, flag in enumerate(direction)
        )
        extended = extended.at[target].set(halos[direction][0])

    shifted = jnp.stack(
        [
            extended[dx : dx + size_x, dy : dy + size_y, dz : dz + size_z]
            for dx, dy, dz in OFFSETS
        ]
    ).reshape((2, 2, 2, size_x, size_y, size_z, channels_in))
    parities = jnp.einsum(
        "xyzabci,xpyqzroi->apbqcro",
        shifted,
        forward_weight(weight_late),
        preferred_element_type=jnp.float32,
    )
    up = parities.reshape(fine_x, fine_y, fine_z, channels_out)
    fine = fine_keep.astype(jnp.float32) * (
        skip.reshape(fine_x, fine_y, fine_z, channels_out).astype(jnp.float32) + up
    )
    fine_out = fine.astype(jnp.bfloat16).reshape(skip.shape)

    scale = 1.0 / math.sqrt(regions * lax.axis_size("chip") * lax.axis_size("core") * size_x * size_y * size_z)
    weight_grad, (fine_out, coarse_grad) = all_spread(
        reduced * scale, plan, (fine_out, coarse_grad)
    )
    return (fine_out, coarse_grad, weight_grad)


def solution(mesh):
    brick, batch = mesh.shape["brick"], mesh.shape["batch"]
    pairs = Mesh(
        mesh.devices.reshape(brick, batch // 2, 2), ("brick", "chip", "core")
    )
    in_specs = (
        P(BATCH, "brick", None, None, None),
        P(BATCH, "brick", None),
        P(BATCH, "brick", None, None, None),
        P(BATCH, "brick", None),
        P(),
        P(BATCH, "brick", None, None, None),
    )
    out_specs = (P(BATCH, "brick", None, None, None), P(BATCH, "brick", None, None, None), P())
    return jax.shard_map(body, mesh=pairs, in_specs=in_specs, out_specs=out_specs, check_vma=False)
```

```python
import math

import jax
import jax.numpy as jnp
from jax import lax
from jax.sharding import Mesh, PartitionSpec as P

OFFSETS = tuple((dx, dy, dz) for dx in range(2) for dy in range(2) for dz in range(2))
DIRECTIONS = OFFSETS[1:]
BATCH = ("chip", "core")
OTHERS = ("brick", "chip")


def region_of(rank):
    return (rank // 4, rank // 2 % 2, rank % 2)


def neighbour_pairs(regions, direction, sign):
    grid = (regions // 4, 2, 2)
    pairs = []
    for dst in range(regions):
        spot = region_of(dst)
        src = tuple(spot[a] + sign * direction[a] for a in range(3))
        if all(0 <= src[a] < grid[a] for a in range(3)):
            pairs.append((4 * src[0] + 2 * src[1] + src[2], dst))
    return pairs


def exchange(piece, regions, direction, sign):
    pairs = neighbour_pairs(regions, direction, sign)
    if not pairs:
        return jnp.zeros_like(piece)
    return lax.ppermute(piece, "brick", pairs)


def halo_exchange(masked_piece, cot_piece, regions, direction):
    down = neighbour_pairs(regions, direction, 1)
    up = neighbour_pairs(regions, direction, -1)
    both = down + up
    sources = [a for a, _ in both]
    targets = [b for _, b in both]
    if not both or len(set(sources)) < len(both) or len(set(targets)) < len(both):
        return (
            exchange(masked_piece, regions, direction, 1),
            exchange(cot_piece, regions, direction, -1),
        )
    spot = region_of(lax.axis_index("brick"))
    grid = (regions // 4, 2, 2)
    sends_down = jnp.bool_(True)
    sends_up = jnp.bool_(True)
    for a in range(3):
        if direction[a]:
            sends_down = sends_down & (spot[a] >= 1)
            sends_up = sends_up & (spot[a] + 1 < grid[a])
    cut = masked_piece.size
    zero = jnp.zeros((), masked_piece.dtype)
    packed = jnp.concatenate(
        [
            jnp.where(sends_down, masked_piece.reshape(-1), zero),
            jnp.where(sends_up, cot_piece.reshape(-1), zero),
        ]
    )
    got = lax.ppermute(packed, "brick", both)
    return (got[:cut].reshape(masked_piece.shape), got[cut:].reshape(cot_piece.shape))


def forward_weight(up_weight):
    channels = up_weight.shape[1:]
    taps = jnp.pad(up_weight.reshape((3, 3, 3) + channels), ((0, 1), (0, 1), (0, 1), (0, 0), (0, 0)))
    for axis in range(3):
        taps = jnp.roll(taps, -1, axis=axis)
    return taps.reshape((2, 2, 2, 2, 2, 2) + channels)


def all_reduce(half):
    devices = lax.axis_size("brick") * lax.axis_size("chip")
    lanes = half.shape[-1]
    rows = half.reshape(-1, lanes)
    size = rows.shape[0]
    chunk = -(-size // (devices * 8)) * 8
    rows = jnp.pad(rows, ((0, chunk * devices - size), (0, 0)))
    parts = lax.all_to_all(rows.reshape(devices, chunk, lanes), OTHERS, 0, 0, tiled=True)
    return parts.sum(axis=0), (devices, chunk, size, half.shape)


def all_spread(reduced, plan, riders):
    devices, chunk, size, shape = plan
    spread = jnp.broadcast_to(reduced[None], (devices,) + reduced.shape)
    half = lax.all_to_all(spread, OTHERS, 0, 0, tiled=True)
    half, riders = lax.optimization_barrier((half, riders))
    half = half.reshape(-1, reduced.shape[-1])[:size].reshape(shape)
    other = lax.ppermute(half, "core", [(0, 1), (1, 0)])
    three = jnp.stack([half, other, half], axis=1)
    whole = lax.dynamic_slice_in_dim(three, lax.axis_index("core"), 2, axis=1)
    return whole.reshape(shape[0], 2 * shape[1], shape[2]), riders


def body(coarse, coarse_mask, skip, fine_mask, up_weight, fine_grad):
    regions = lax.axis_size("brick")
    size_x, size_y, merged = coarse.shape[2:]
    channels_out = up_weight.shape[1]
    channels_in = up_weight.shape[2]
    size_z = merged // channels_in
    fine_x, fine_y, fine_merged = skip.shape[2:]
    fine_z = fine_merged // channels_out
    counts = (size_x, size_y, size_z)

    coarse_keep = coarse_mask.reshape(size_x, size_y, size_z, 1).astype(jnp.bfloat16)
    masked = coarse.reshape(size_x, size_y, size_z, channels_in) * coarse_keep
    fine_keep = fine_mask.reshape(fine_x, fine_y, fine_z, 1)
    cotangent = fine_grad.reshape(fine_x, fine_y, fine_z, channels_out) * fine_keep.astype(
        jnp.bfloat16
    )

    halos = {}
    for direction in DIRECTIONS:
        masked_piece = masked[tuple(slice(0, 1) if flag else slice(None) for flag in direction)]
        cot_piece = cotangent[tuple(slice(-1, None) if flag else slice(None) for flag in direction)]
        halos[direction] = halo_exchange(masked_piece, cot_piece, regions, direction)
    widened = jnp.pad(cotangent, ((1, 1), (1, 1), (1, 1), (0, 0)))
    for direction in DIRECTIONS:
        target = tuple(
            slice(0, 1) if flag else slice(1, 1 + cotangent.shape[a])
            for a, flag in enumerate(direction)
        )
        widened = widened.at[target].set(halos[direction][1])
    window = tuple(2 * c + 1 for c in counts)
    trimmed = widened[: window[0], : window[1], : window[2]]
    full = lax.conv_general_dilated(
        trimmed[..., None],
        masked[..., None],
        (1, 1, 1),
        "VALID",
        rhs_dilation=(2, 2, 2),
        dimension_numbers=("XYZNC", "XYZOI", "XYZNC"),
        preferred_element_type=jnp.float32,
    ).reshape(27, channels_out, channels_in)
    core = lax.axis_index("core")
    share = channels_out // 2
    theirs = lax.dynamic_slice_in_dim(full, (1 - core) * share, share, axis=1)
    got = lax.ppermute(theirs, "core", [(0, 1), (1, 0)])
    grads = lax.dynamic_slice_in_dim(full, core * share, share, axis=1) + got
    grads, masked_late, weight_late, skip, fine_keep = lax.optimization_barrier(
        (grads, masked, up_weight, skip, fine_keep)
    )
    reduced, plan = all_reduce(grads)

    back = lax.conv_general_dilated(
        widened[None, : window[0], : window[1], : window[2]],
        up_weight.reshape((3, 3, 3, channels_out, channels_in)),
        (2, 2, 2),
        "VALID",
        dimension_numbers=("NXYZC", "XYZIO", "NXYZC"),
        preferred_element_type=jnp.float32,
    )[0]
    coarse_grad = (
        (back * coarse_keep.astype(jnp.float32)).astype(jnp.bfloat16).reshape(coarse.shape)
    )

    extended = jnp.pad(masked_late, ((0, 1), (0, 1), (0, 1), (0, 0)))
    for direction in DIRECTIONS:
        target = tuple(
            slice(counts[a], counts[a] + 1) if flag else slice(0, counts[a])
            for a, flag in enumerate(direction)
        )
        extended = extended.at[target].set(halos[direction][0])

    shifted = jnp.stack(
        [
            extended[dx : dx + size_x, dy : dy + size_y, dz : dz + size_z]
            for dx, dy, dz in OFFSETS
        ]
    ).reshape((2, 2, 2, size_x, size_y, size_z, channels_in))
    parities = jnp.einsum(
        "xyzabci,xpyqzroi->apbqcro",
        shifted,
        forward_weight(weight_late),
        preferred_element_type=jnp.float32,
    )
    up = parities.reshape(fine_x, fine_y, fine_z, channels_out)
    fine = fine_keep.astype(jnp.float32) * (
        skip.reshape(fine_x, fine_y, fine_z, channels_out).astype(jnp.float32) + up
    )
    fine_out = fine.astype(jnp.bfloat16).reshape(skip.shape)

    scale = 1.0 / math.sqrt(regions * lax.axis_size("chip") * lax.axis_size("core") * size_x * size_y * size_z)
    weight_grad, (fine_out, coarse_grad) = all_spread(
        reduced * scale, plan, (fine_out, coarse_grad)
    )
    return (fine_out, coarse_grad, weight_grad)


def solution(mesh):
    brick, batch = mesh.shape["brick"], mesh.shape["batch"]
    pairs = Mesh(
        mesh.devices.reshape(brick, batch // 2, 2), ("brick", "chip", "core")
    )
    in_specs = (
        P(BATCH, "brick", None, None, None),
        P(BATCH, "brick", None),
        P(BATCH, "brick", None, None, None),
        P(BATCH, "brick", None),
        P(),
        P(BATCH, "brick", None, None, None),
    )
    out_specs = (P(BATCH, "brick", None, None, None), P(BATCH, "brick", None, None, None), P())
    return jax.shard_map(body, mesh=pairs, in_specs=in_specs, out_specs=out_specs, check_vma=False)
```

```python
import math

import jax
import jax.numpy as jnp
from jax import lax
from jax.sharding import Mesh, PartitionSpec as P

OFFSETS = tuple((dx, dy, dz) for dx in range(2) for dy in range(2) for dz in range(2))
DIRECTIONS = OFFSETS[1:]
BATCH = ("chip", "core")
OTHERS = ("brick", "chip")


def region_of(rank):
    return (rank // 4, rank // 2 % 2, rank % 2)


def neighbour_pairs(regions, direction, sign):
    grid = (regions // 4, 2, 2)
    pairs = []
    for dst in range(regions):
        spot = region_of(dst)
        src = tuple(spot[a] + sign * direction[a] for a in range(3))
        if all(0 <= src[a] < grid[a] for a in range(3)):
            pairs.append((4 * src[0] + 2 * src[1] + src[2], dst))
    return pairs


def exchange(piece, regions, direction, sign):
    pairs = neighbour_pairs(regions, direction, sign)
    if not pairs:
        return jnp.zeros_like(piece)
    return lax.ppermute(piece, "brick", pairs)


def halo_exchange(masked_piece, cot_piece, regions, direction):
    down = neighbour_pairs(regions, direction, 1)
    up = neighbour_pairs(regions, direction, -1)
    both = down + up
    sources = [a for a, _ in both]
    targets = [b for _, b in both]
    if not both or len(set(sources)) < len(both) or len(set(targets)) < len(both):
        return (
            exchange(masked_piece, regions, direction, 1),
            exchange(cot_piece, regions, direction, -1),
        )
    spot = region_of(lax.axis_index("brick"))
    grid = (regions // 4, 2, 2)
    sends_down = jnp.bool_(True)
    sends_up = jnp.bool_(True)
    for a in range(3):
        if direction[a]:
            sends_down = sends_down & (spot[a] >= 1)
            sends_up = sends_up & (spot[a] + 1 < grid[a])
    cut = masked_piece.size
    zero = jnp.zeros((), masked_piece.dtype)
    packed = jnp.concatenate(
        [
            jnp.where(sends_down, masked_piece.reshape(-1), zero),
            jnp.where(sends_up, cot_piece.reshape(-1), zero),
        ]
    )
    got = lax.ppermute(packed, "brick", both)
    return (got[:cut].reshape(masked_piece.shape), got[cut:].reshape(cot_piece.shape))


def all_reduce(half):
    devices = lax.axis_size("brick") * lax.axis_size("chip")
    lanes = half.shape[-1]
    rows = half.reshape(-1, lanes)
    size = rows.shape[0]
    chunk = -(-size // (devices * 8)) * 8
    rows = jnp.pad(rows, ((0, chunk * devices - size), (0, 0)))
    parts = lax.all_to_all(rows.reshape(devices, chunk, lanes), OTHERS, 0, 0, tiled=True)
    return parts.sum(axis=0), (devices, chunk, size, half.shape)


def all_spread(reduced, plan, riders):
    devices, chunk, size, shape = plan
    spread = jnp.broadcast_to(reduced[None], (devices,) + reduced.shape)
    half = lax.all_to_all(spread, OTHERS, 0, 0, tiled=True)
    half, riders = lax.optimization_barrier((half, riders))
    half = half.reshape(-1, reduced.shape[-1])[:size].reshape(shape)
    other = lax.ppermute(half, "core", [(0, 1), (1, 0)])
    three = jnp.stack([half, other, half], axis=1)
    whole = lax.dynamic_slice_in_dim(three, lax.axis_index("core"), 2, axis=1)
    return whole.reshape(shape[0], 2 * shape[1], shape[2]), riders


def body(coarse, coarse_mask, skip, fine_mask, up_weight, fine_grad):
    regions = lax.axis_size("brick")
    size_x, size_y, merged = coarse.shape[2:]
    channels_out = up_weight.shape[1]
    channels_in = up_weight.shape[2]
    size_z = merged // channels_in
    fine_x, fine_y, fine_merged = skip.shape[2:]
    fine_z = fine_merged // channels_out
    counts = (size_x, size_y, size_z)

    coarse_keep = coarse_mask.reshape(size_x, size_y, size_z, 1).astype(jnp.bfloat16)
    masked = coarse.reshape(size_x, size_y, size_z, channels_in) * coarse_keep
    fine_keep = fine_mask.reshape(fine_x, fine_y, fine_z, 1)
    cotangent = fine_grad.reshape(fine_x, fine_y, fine_z, channels_out) * fine_keep.astype(
        jnp.bfloat16
    )

    halos = {}
    for direction in DIRECTIONS:
        masked_piece = masked[tuple(slice(0, 1) if flag else slice(None) for flag in direction)]
        cot_piece = cotangent[tuple(slice(-1, None) if flag else slice(None) for flag in direction)]
        halos[direction] = halo_exchange(masked_piece, cot_piece, regions, direction)
    widened = jnp.pad(cotangent, ((1, 1), (1, 1), (1, 1), (0, 0)))
    for direction in DIRECTIONS:
        target = tuple(
            slice(0, 1) if flag else slice(1, 1 + cotangent.shape[a])
            for a, flag in enumerate(direction)
        )
        widened = widened.at[target].set(halos[direction][1])
    window = tuple(2 * c + 1 for c in counts)
    trimmed = widened[: window[0], : window[1], : window[2]]
    full = lax.conv_general_dilated(
        trimmed[..., None],
        masked[..., None],
        (1, 1, 1),
        "VALID",
        rhs_dilation=(2, 2, 2),
        dimension_numbers=("XYZNC", "XYZOI", "XYZNC"),
        preferred_element_type=jnp.float32,
    ).reshape(27, channels_out, channels_in)
    core = lax.axis_index("core")
    share = channels_out // 2
    theirs = lax.dynamic_slice_in_dim(full, (1 - core) * share, share, axis=1)
    got = lax.ppermute(theirs, "core", [(0, 1), (1, 0)])
    grads = lax.dynamic_slice_in_dim(full, core * share, share, axis=1) + got
    grads, masked_late, weight_late, skip, fine_keep = lax.optimization_barrier(
        (grads, masked, up_weight, skip, fine_keep)
    )
    reduced, plan = all_reduce(grads)

    back = lax.conv_general_dilated(
        widened[None, : window[0], : window[1], : window[2]],
        up_weight.reshape((3, 3, 3, channels_out, channels_in)),
        (2, 2, 2),
        "VALID",
        dimension_numbers=("NXYZC", "XYZIO", "NXYZC"),
        preferred_element_type=jnp.float32,
    )[0]
    coarse_grad = (
        (back * coarse_keep.astype(jnp.float32)).astype(jnp.bfloat16).reshape(coarse.shape)
    )

    extended = jnp.pad(masked_late, ((0, 1), (0, 1), (0, 1), (0, 0)))
    for direction in DIRECTIONS:
        target = tuple(
            slice(counts[a], counts[a] + 1) if flag else slice(0, counts[a])
            for a, flag in enumerate(direction)
        )
        extended = extended.at[target].set(halos[direction][0])

    flipped = weight_late.reshape((3, 3, 3, channels_out, channels_in))[::-1, ::-1, ::-1]
    up = lax.conv_general_dilated(
        extended[None],
        flipped,
        (1, 1, 1),
        ((1, 0), (1, 0), (1, 0)),
        lhs_dilation=(2, 2, 2),
        dimension_numbers=("NXYZC", "XYZOI", "NXYZC"),
        preferred_element_type=jnp.float32,
    )[0]
    fine = fine_keep.astype(jnp.float32) * (
        skip.reshape(fine_x, fine_y, fine_z, channels_out).astype(jnp.float32) + up
    )
    fine_out = fine.astype(jnp.bfloat16).reshape(skip.shape)

    scale = 1.0 / math.sqrt(regions * lax.axis_size("chip") * lax.axis_size("core") * size_x * size_y * size_z)
    weight_grad, (fine_out, coarse_grad) = all_spread(
        reduced * scale, plan, (fine_out, coarse_grad)
    )
    return (fine_out, coarse_grad, weight_grad)


def solution(mesh):
    brick, batch = mesh.shape["brick"], mesh.shape["batch"]
    pairs = Mesh(
        mesh.devices.reshape(brick, batch // 2, 2), ("brick", "chip", "core")
    )
    in_specs = (
        P(BATCH, "brick", None, None, None),
        P(BATCH, "brick", None),
        P(BATCH, "brick", None, None, None),
        P(BATCH, "brick", None),
        P(),
        P(BATCH, "brick", None, None, None),
    )
    out_specs = (P(BATCH, "brick", None, None, None), P(BATCH, "brick", None, None, None), P())
    return jax.shard_map(body, mesh=pairs, in_specs=in_specs, out_specs=out_specs, check_vma=False)
```

```python
import math

import jax
import jax.numpy as jnp
from jax import lax
from jax.sharding import Mesh, PartitionSpec as P

OFFSETS = tuple((dx, dy, dz) for dx in range(2) for dy in range(2) for dz in range(2))
DIRECTIONS = OFFSETS[1:]
BATCH = ("chip", "core")
OTHERS = ("brick", "chip")


def region_of(rank):
    return (rank // 4, rank // 2 % 2, rank % 2)


def neighbour_pairs(regions, direction, sign):
    grid = (regions // 4, 2, 2)
    pairs = []
    for dst in range(regions):
        spot = region_of(dst)
        src = tuple(spot[a] + sign * direction[a] for a in range(3))
        if all(0 <= src[a] < grid[a] for a in range(3)):
            pairs.append((4 * src[0] + 2 * src[1] + src[2], dst))
    return pairs


def exchange(piece, regions, direction, sign):
    pairs = neighbour_pairs(regions, direction, sign)
    if not pairs:
        return jnp.zeros_like(piece)
    return lax.ppermute(piece, "brick", pairs)


def halo_exchange(masked_piece, cot_piece, regions, direction):
    down = neighbour_pairs(regions, direction, 1)
    up = neighbour_pairs(regions, direction, -1)
    both = down + up
    sources = [a for a, _ in both]
    targets = [b for _, b in both]
    if not both or len(set(sources)) < len(both) or len(set(targets)) < len(both):
        return (
            exchange(masked_piece, regions, direction, 1),
            exchange(cot_piece, regions, direction, -1),
        )
    spot = region_of(lax.axis_index("brick"))
    grid = (regions // 4, 2, 2)
    sends_down = jnp.bool_(True)
    sends_up = jnp.bool_(True)
    for a in range(3):
        if direction[a]:
            sends_down = sends_down & (spot[a] >= 1)
            sends_up = sends_up & (spot[a] + 1 < grid[a])
    cut = masked_piece.size
    zero = jnp.zeros((), masked_piece.dtype)
    packed = jnp.concatenate(
        [
            jnp.where(sends_down, masked_piece.reshape(-1), zero),
            jnp.where(sends_up, cot_piece.reshape(-1), zero),
        ]
    )
    got = lax.ppermute(packed, "brick", both)
    return (got[:cut].reshape(masked_piece.shape), got[cut:].reshape(cot_piece.shape))


def all_reduce(half):
    devices = lax.axis_size("brick") * lax.axis_size("chip")
    lanes = half.shape[-1]
    rows = half.reshape(-1, lanes)
    size = rows.shape[0]
    chunk = -(-size // (devices * 8)) * 8
    rows = jnp.pad(rows, ((0, chunk * devices - size), (0, 0)))
    parts = lax.all_to_all(rows.reshape(devices, chunk, lanes), OTHERS, 0, 0, tiled=True)
    return parts.sum(axis=0), (devices, chunk, size, half.shape)


def all_spread(reduced, plan, riders):
    devices, chunk, size, shape = plan
    spread = jnp.broadcast_to(reduced[None], (devices,) + reduced.shape)
    half = lax.all_to_all(spread, OTHERS, 0, 0, tiled=True)
    half, riders = lax.optimization_barrier((half, riders))
    half = half.reshape(-1, reduced.shape[-1])[:size].reshape(shape)
    other = lax.ppermute(half, "core", [(0, 1), (1, 0)])
    core = lax.axis_index("core")
    whole = jnp.zeros((shape[0], 2) + shape[1:], half.dtype)
    whole = lax.dynamic_update_index_in_dim(whole, half, core, 1)
    whole = lax.dynamic_update_index_in_dim(whole, other, 1 - core, 1)
    return whole.reshape(shape[0], 2 * shape[1], shape[2]), riders


def body(coarse, coarse_mask, skip, fine_mask, up_weight, fine_grad):
    regions = lax.axis_size("brick")
    size_x, size_y, merged = coarse.shape[2:]
    channels_out = up_weight.shape[1]
    channels_in = up_weight.shape[2]
    size_z = merged // channels_in
    fine_x, fine_y, fine_merged = skip.shape[2:]
    fine_z = fine_merged // channels_out
    counts = (size_x, size_y, size_z)

    coarse_keep = coarse_mask.reshape(size_x, size_y, size_z, 1).astype(jnp.bfloat16)
    masked = coarse.reshape(size_x, size_y, size_z, channels_in) * coarse_keep
    fine_keep = fine_mask.reshape(fine_x, fine_y, fine_z, 1)
    cotangent = fine_grad.reshape(fine_x, fine_y, fine_z, channels_out) * fine_keep.astype(
        jnp.bfloat16
    )

    halos = {}
    for direction in DIRECTIONS:
        masked_piece = masked[tuple(slice(0, 1) if flag else slice(None) for flag in direction)]
        cot_piece = cotangent[tuple(slice(-1, None) if flag else slice(None) for flag in direction)]
        halos[direction] = halo_exchange(masked_piece, cot_piece, regions, direction)
    widened = jnp.pad(cotangent, ((1, 0), (1, 0), (1, 0), (0, 0)))
    for direction in DIRECTIONS:
        target = tuple(
            slice(0, 1) if flag else slice(1, 1 + cotangent.shape[a])
            for a, flag in enumerate(direction)
        )
        widened = widened.at[target].set(halos[direction][1])
    full = lax.conv_general_dilated(
        widened[..., None],
        masked[..., None],
        (1, 1, 1),
        "VALID",
        rhs_dilation=(2, 2, 2),
        dimension_numbers=("XYZNC", "XYZOI", "XYZNC"),
        preferred_element_type=jnp.float32,
    ).reshape(27, channels_out, channels_in)
    core = lax.axis_index("core")
    share = channels_out // 2
    theirs = lax.dynamic_slice_in_dim(full, (1 - core) * share, share, axis=1)
    got = lax.ppermute(theirs, "core", [(0, 1), (1, 0)])
    grads = lax.dynamic_slice_in_dim(full, core * share, share, axis=1) + got
    grads, masked_late, weight_late, skip, fine_keep = lax.optimization_barrier(
        (grads, masked, up_weight, skip, fine_keep)
    )
    reduced, plan = all_reduce(grads)

    back = lax.conv_general_dilated(
        widened[None],
        up_weight.reshape((3, 3, 3, channels_out, channels_in)),
        (2, 2, 2),
        "VALID",
        dimension_numbers=("NXYZC", "XYZIO", "NXYZC"),
        preferred_element_type=jnp.float32,
    )[0]
    coarse_grad = (
        (back * coarse_keep.astype(jnp.float32)).astype(jnp.bfloat16).reshape(coarse.shape)
    )

    extended = jnp.pad(masked_late, ((0, 1), (0, 1), (0, 1), (0, 0)))
    for direction in DIRECTIONS:
        target = tuple(
            slice(counts[a], counts[a] + 1) if flag else slice(0, counts[a])
            for a, flag in enumerate(direction)
        )
        extended = extended.at[target].set(halos[direction][0])

    flipped = weight_late.reshape((3, 3, 3, channels_out, channels_in))[::-1, ::-1, ::-1]
    up = lax.conv_general_dilated(
        extended[None],
        flipped,
        (1, 1, 1),
        ((1, 0), (1, 0), (1, 0)),
        lhs_dilation=(2, 2, 2),
        dimension_numbers=("NXYZC", "XYZOI", "NXYZC"),
        preferred_element_type=jnp.float32,
    )[0]
    fine = fine_keep.astype(jnp.float32) * (
        skip.reshape(fine_x, fine_y, fine_z, channels_out).astype(jnp.float32) + up
    )
    fine_out = fine.astype(jnp.bfloat16).reshape(skip.shape)

    scale = 1.0 / math.sqrt(regions * lax.axis_size("chip") * lax.axis_size("core") * size_x * size_y * size_z)
    weight_grad, (fine_out, coarse_grad) = all_spread(
        reduced * scale, plan, (fine_out, coarse_grad)
    )
    return (fine_out, coarse_grad, weight_grad)


def solution(mesh):
    brick, batch = mesh.shape["brick"], mesh.shape["batch"]
    pairs = Mesh(
        mesh.devices.reshape(brick, batch // 2, 2), ("brick", "chip", "core")
    )
    in_specs = (
        P(BATCH, "brick", None, None, None),
        P(BATCH, "brick", None),
        P(BATCH, "brick", None, None, None),
        P(BATCH, "brick", None),
        P(),
        P(BATCH, "brick", None, None, None),
    )
    out_specs = (P(BATCH, "brick", None, None, None), P(BATCH, "brick", None, None, None), P())
    return jax.shard_map(body, mesh=pairs, in_specs=in_specs, out_specs=out_specs, check_vma=False)
```

```python
import math

import jax
import jax.numpy as jnp
from jax import lax
from jax.sharding import Mesh, PartitionSpec as P

OFFSETS = tuple((dx, dy, dz) for dx in range(2) for dy in range(2) for dz in range(2))
DIRECTIONS = OFFSETS[1:]
BATCH = ("chip", "core")
OTHERS = ("brick", "chip")


def region_of(rank):
    return (rank // 4, rank // 2 % 2, rank % 2)


def neighbour_pairs(regions, direction, sign):
    grid = (regions // 4, 2, 2)
    pairs = []
    for dst in range(regions):
        spot = region_of(dst)
        src = tuple(spot[a] + sign * direction[a] for a in range(3))
        if all(0 <= src[a] < grid[a] for a in range(3)):
            pairs.append((4 * src[0] + 2 * src[1] + src[2], dst))
    return pairs


def exchange(piece, regions, direction, sign):
    pairs = neighbour_pairs(regions, direction, sign)
    if not pairs:
        return jnp.zeros_like(piece)
    return lax.ppermute(piece, "brick", pairs)


def halo_exchange(masked_piece, cot_piece, regions, direction):
    down = neighbour_pairs(regions, direction, 1)
    up = neighbour_pairs(regions, direction, -1)
    both = down + up
    sources = [a for a, _ in both]
    targets = [b for _, b in both]
    if not both or len(set(sources)) < len(both) or len(set(targets)) < len(both):
        return (
            exchange(masked_piece, regions, direction, 1),
            exchange(cot_piece, regions, direction, -1),
        )
    spot = region_of(lax.axis_index("brick"))
    grid = (regions // 4, 2, 2)
    sends_down = jnp.bool_(True)
    sends_up = jnp.bool_(True)
    for a in range(3):
        if direction[a]:
            sends_down = sends_down & (spot[a] >= 1)
            sends_up = sends_up & (spot[a] + 1 < grid[a])
    cut = masked_piece.size
    zero = jnp.zeros((), masked_piece.dtype)
    packed = jnp.concatenate(
        [
            jnp.where(sends_down, masked_piece.reshape(-1), zero),
            jnp.where(sends_up, cot_piece.reshape(-1), zero),
        ]
    )
    got = lax.ppermute(packed, "brick", both)
    return (got[:cut].reshape(masked_piece.shape), got[cut:].reshape(cot_piece.shape))


def all_reduce(half):
    devices = lax.axis_size("brick") * lax.axis_size("chip")
    lanes = half.shape[-1]
    rows = half.reshape(-1, lanes)
    size = rows.shape[0]
    chunk = -(-size // (devices * 8)) * 8
    rows = jnp.pad(rows, ((0, chunk * devices - size), (0, 0)))
    parts = lax.all_to_all(rows.reshape(devices, chunk, lanes), OTHERS, 0, 0, tiled=True)
    return parts.sum(axis=0), (devices, chunk, size, half.shape)


def all_spread(reduced, plan, riders):
    devices, chunk, size, shape = plan
    spread = jnp.broadcast_to(reduced[None], (devices,) + reduced.shape)
    half = lax.all_to_all(spread, OTHERS, 0, 0, tiled=True)
    half, riders = lax.optimization_barrier((half, riders))
    half = half.reshape(-1, reduced.shape[-1])[:size].reshape(shape)
    other = lax.ppermute(half, "core", [(0, 1), (1, 0)])
    core = lax.axis_index("core")
    whole = jnp.zeros((shape[0], 2) + shape[1:], half.dtype)
    whole = lax.dynamic_update_index_in_dim(whole, half, core, 1)
    whole = lax.dynamic_update_index_in_dim(whole, other, 1 - core, 1)
    return whole.reshape(shape[0], 2 * shape[1], shape[2]), riders


def body(coarse, coarse_mask, skip, fine_mask, up_weight, fine_grad):
    regions = lax.axis_size("brick")
    size_x, size_y, merged = coarse.shape[2:]
    channels_out = up_weight.shape[1]
    channels_in = up_weight.shape[2]
    size_z = merged // channels_in
    fine_x, fine_y, fine_merged = skip.shape[2:]
    fine_z = fine_merged // channels_out
    counts = (size_x, size_y, size_z)

    coarse_keep = coarse_mask.reshape(size_x, size_y, size_z, 1).astype(jnp.bfloat16)
    masked = coarse.reshape(size_x, size_y, size_z, channels_in) * coarse_keep
    fine_keep = fine_mask.reshape(fine_x, fine_y, fine_z, 1)
    cotangent = fine_grad.reshape(fine_x, fine_y, fine_z, channels_out) * fine_keep.astype(
        jnp.bfloat16
    )

    extended = masked
    widened = cotangent
    for axis in (2, 1, 0):
        direction = tuple(1 if other == axis else 0 for other in range(3))
        last = widened.shape[axis]
        got_masked, got_cot = halo_exchange(
            lax.slice_in_dim(extended, 0, 1, axis=axis),
            lax.slice_in_dim(widened, last - 1, last, axis=axis),
            regions,
            direction,
        )
        extended = jnp.concatenate([extended, got_masked], axis=axis)
        widened = jnp.concatenate([got_cot, widened], axis=axis)
    full = lax.conv_general_dilated(
        widened[..., None],
        masked[..., None],
        (1, 1, 1),
        "VALID",
        rhs_dilation=(2, 2, 2),
        dimension_numbers=("XYZNC", "XYZOI", "XYZNC"),
        preferred_element_type=jnp.float32,
    ).reshape(27, channels_out, channels_in)
    core = lax.axis_index("core")
    share = channels_out // 2
    theirs = lax.dynamic_slice_in_dim(full, (1 - core) * share, share, axis=1)
    got = lax.ppermute(theirs, "core", [(0, 1), (1, 0)])
    grads = lax.dynamic_slice_in_dim(full, core * share, share, axis=1) + got
    grads, extended, weight_late, skip, fine_keep = lax.optimization_barrier(
        (grads, extended, up_weight, skip, fine_keep)
    )
    reduced, plan = all_reduce(grads)

    back = lax.conv_general_dilated(
        widened[None],
        up_weight.reshape((3, 3, 3, channels_out, channels_in)),
        (2, 2, 2),
        "VALID",
        dimension_numbers=("NXYZC", "XYZIO", "NXYZC"),
        preferred_element_type=jnp.float32,
    )[0]
    coarse_grad = (
        (back * coarse_keep.astype(jnp.float32)).astype(jnp.bfloat16).reshape(coarse.shape)
    )

    flipped = weight_late.reshape((3, 3, 3, channels_out, channels_in))[::-1, ::-1, ::-1]
    up = lax.conv_general_dilated(
        extended[None],
        flipped,
        (1, 1, 1),
        ((1, 0), (1, 0), (1, 0)),
        lhs_dilation=(2, 2, 2),
        dimension_numbers=("NXYZC", "XYZOI", "NXYZC"),
        preferred_element_type=jnp.float32,
    )[0]
    fine = fine_keep.astype(jnp.float32) * (
        skip.reshape(fine_x, fine_y, fine_z, channels_out).astype(jnp.float32) + up
    )
    fine_out = fine.astype(jnp.bfloat16).reshape(skip.shape)

    scale = 1.0 / math.sqrt(regions * lax.axis_size("chip") * lax.axis_size("core") * size_x * size_y * size_z)
    weight_grad, (fine_out, coarse_grad) = all_spread(
        reduced * scale, plan, (fine_out, coarse_grad)
    )
    return (fine_out, coarse_grad, weight_grad)


def solution(mesh):
    brick, batch = mesh.shape["brick"], mesh.shape["batch"]
    pairs = Mesh(
        mesh.devices.reshape(brick, batch // 2, 2), ("brick", "chip", "core")
    )
    in_specs = (
        P(BATCH, "brick", None, None, None),
        P(BATCH, "brick", None),
        P(BATCH, "brick", None, None, None),
        P(BATCH, "brick", None),
        P(),
        P(BATCH, "brick", None, None, None),
    )
    out_specs = (P(BATCH, "brick", None, None, None), P(BATCH, "brick", None, None, None), P())
    return jax.shard_map(body, mesh=pairs, in_specs=in_specs, out_specs=out_specs, check_vma=False)
```

```python
import math

import jax
import jax.numpy as jnp
from jax import lax
from jax.sharding import Mesh, PartitionSpec as P

OFFSETS = tuple((dx, dy, dz) for dx in range(2) for dy in range(2) for dz in range(2))
DIRECTIONS = OFFSETS[1:]
BATCH = ("chip", "core")
OTHERS = ("brick", "chip")


def region_of(rank):
    return (rank // 4, rank // 2 % 2, rank % 2)


def neighbour_pairs(regions, direction, sign):
    grid = (regions // 4, 2, 2)
    pairs = []
    for dst in range(regions):
        spot = region_of(dst)
        src = tuple(spot[a] + sign * direction[a] for a in range(3))
        if all(0 <= src[a] < grid[a] for a in range(3)):
            pairs.append((4 * src[0] + 2 * src[1] + src[2], dst))
    return pairs


def exchange(piece, regions, direction, sign):
    pairs = neighbour_pairs(regions, direction, sign)
    if not pairs:
        return jnp.zeros_like(piece)
    return lax.ppermute(piece, "brick", pairs)


def halo_exchange(masked_piece, cot_piece, regions, direction):
    down = neighbour_pairs(regions, direction, 1)
    up = neighbour_pairs(regions, direction, -1)
    both = down + up
    sources = [a for a, _ in both]
    targets = [b for _, b in both]
    if not both or len(set(sources)) < len(both) or len(set(targets)) < len(both):
        return (
            exchange(masked_piece, regions, direction, 1),
            exchange(cot_piece, regions, direction, -1),
        )
    spot = region_of(lax.axis_index("brick"))
    grid = (regions // 4, 2, 2)
    sends_down = jnp.bool_(True)
    sends_up = jnp.bool_(True)
    for a in range(3):
        if direction[a]:
            sends_down = sends_down & (spot[a] >= 1)
            sends_up = sends_up & (spot[a] + 1 < grid[a])
    cut = masked_piece.size
    zero = jnp.zeros((), masked_piece.dtype)
    packed = jnp.concatenate(
        [
            jnp.where(sends_down, masked_piece.reshape(-1), zero),
            jnp.where(sends_up, cot_piece.reshape(-1), zero),
        ]
    )
    got = lax.ppermute(packed, "brick", both)
    return (got[:cut].reshape(masked_piece.shape), got[cut:].reshape(cot_piece.shape))


def all_reduce(half, taps):
    devices = lax.axis_size("brick") * lax.axis_size("chip")
    lanes = half.shape[-1]
    rows = half.reshape(-1, lanes)
    chunk = rows.shape[0] // devices
    parts = lax.all_to_all(rows.reshape(devices, chunk, lanes), OTHERS, 0, 0, tiled=True)
    return parts.sum(axis=0), (half.shape, taps)


def all_spread(reduced, plan, riders):
    shape, taps = plan
    devices = lax.axis_size("brick") * lax.axis_size("chip")
    spread = jnp.broadcast_to(reduced[None], (devices,) + reduced.shape)
    half = lax.all_to_all(spread, OTHERS, 0, 0, tiled=True)
    half, riders = lax.optimization_barrier((half, riders))
    half = half.reshape(shape)[:taps]
    other = lax.ppermute(half, "core", [(0, 1), (1, 0)])
    core = lax.axis_index("core")
    whole = jnp.zeros((taps, 2) + shape[1:], half.dtype)
    whole = lax.dynamic_update_index_in_dim(whole, half, core, 1)
    whole = lax.dynamic_update_index_in_dim(whole, other, 1 - core, 1)
    return whole.reshape(taps, 2 * shape[1], shape[2]), riders


def padded_taps(taps, share, devices):
    step = devices * 8 // math.gcd(devices * 8, share)
    return -(-taps // step) * step


def body(coarse, coarse_mask, skip, fine_mask, up_weight, fine_grad):
    regions = lax.axis_size("brick")
    size_x, size_y, merged = coarse.shape[2:]
    channels_out = up_weight.shape[1]
    channels_in = up_weight.shape[2]
    size_z = merged // channels_in
    fine_x, fine_y, fine_merged = skip.shape[2:]
    fine_z = fine_merged // channels_out
    counts = (size_x, size_y, size_z)

    coarse_keep = coarse_mask.reshape(size_x, size_y, size_z, 1).astype(jnp.bfloat16)
    masked = coarse.reshape(size_x, size_y, size_z, channels_in) * coarse_keep
    fine_keep = fine_mask.reshape(fine_x, fine_y, fine_z, 1)
    cotangent = fine_grad.reshape(fine_x, fine_y, fine_z, channels_out) * fine_keep.astype(
        jnp.bfloat16
    )

    extended = masked
    widened = cotangent
    for axis in (2, 1, 0):
        direction = tuple(1 if other == axis else 0 for other in range(3))
        last = widened.shape[axis]
        got_masked, got_cot = halo_exchange(
            lax.slice_in_dim(extended, 0, 1, axis=axis),
            lax.slice_in_dim(widened, last - 1, last, axis=axis),
            regions,
            direction,
        )
        extended = jnp.concatenate([extended, got_masked], axis=axis)
        widened = jnp.concatenate([got_cot, widened], axis=axis)
    full = lax.conv_general_dilated(
        widened[..., None],
        masked[..., None],
        (1, 1, 1),
        "VALID",
        rhs_dilation=(2, 2, 2),
        dimension_numbers=("XYZNC", "XYZOI", "XYZNC"),
        preferred_element_type=jnp.float32,
    ).reshape(27, channels_out, channels_in)
    core = lax.axis_index("core")
    share = channels_out // 2
    spare = padded_taps(full.shape[0], share, regions * lax.axis_size("chip")) - full.shape[0]
    theirs = lax.dynamic_slice_in_dim(full, (1 - core) * share, share, axis=1)
    got = lax.ppermute(
        jnp.pad(theirs, ((0, spare), (0, 0), (0, 0))), "core", [(0, 1), (1, 0)]
    )
    mine = lax.dynamic_slice_in_dim(full, core * share, share, axis=1)
    grads = jnp.pad(mine, ((0, spare), (0, 0), (0, 0))) + got
    grads, extended, weight_late, skip, fine_keep = lax.optimization_barrier(
        (grads, extended, up_weight, skip, fine_keep)
    )
    reduced, plan = all_reduce(grads, full.shape[0])

    back = lax.conv_general_dilated(
        widened[None],
        up_weight.reshape((3, 3, 3, channels_out, channels_in)),
        (2, 2, 2),
        "VALID",
        dimension_numbers=("NXYZC", "XYZIO", "NXYZC"),
        preferred_element_type=jnp.float32,
    )[0]
    coarse_grad = (
        (back * coarse_keep.astype(jnp.float32)).astype(jnp.bfloat16).reshape(coarse.shape)
    )

    flipped = weight_late.reshape((3, 3, 3, channels_out, channels_in))[::-1, ::-1, ::-1]
    up = lax.conv_general_dilated(
        extended[None],
        flipped,
        (1, 1, 1),
        ((1, 0), (1, 0), (1, 0)),
        lhs_dilation=(2, 2, 2),
        dimension_numbers=("NXYZC", "XYZOI", "NXYZC"),
        preferred_element_type=jnp.float32,
    )[0]
    fine = fine_keep.astype(jnp.float32) * (
        skip.reshape(fine_x, fine_y, fine_z, channels_out).astype(jnp.float32) + up
    )
    fine_out = fine.astype(jnp.bfloat16).reshape(skip.shape)

    scale = 1.0 / math.sqrt(regions * lax.axis_size("chip") * lax.axis_size("core") * size_x * size_y * size_z)
    weight_grad, (fine_out, coarse_grad) = all_spread(
        reduced * scale, plan, (fine_out, coarse_grad)
    )
    return (fine_out, coarse_grad, weight_grad)


def solution(mesh):
    brick, batch = mesh.shape["brick"], mesh.shape["batch"]
    pairs = Mesh(
        mesh.devices.reshape(brick, batch // 2, 2), ("brick", "chip", "core")
    )
    in_specs = (
        P(BATCH, "brick", None, None, None),
        P(BATCH, "brick", None),
        P(BATCH, "brick", None, None, None),
        P(BATCH, "brick", None),
        P(),
        P(BATCH, "brick", None, None, None),
    )
    out_specs = (P(BATCH, "brick", None, None, None), P(BATCH, "brick", None, None, None), P())
    return jax.shard_map(body, mesh=pairs, in_specs=in_specs, out_specs=out_specs, check_vma=False)
```

```python
import math

import jax
import jax.numpy as jnp
from jax import lax
from jax.sharding import Mesh, PartitionSpec as P

OFFSETS = tuple((dx, dy, dz) for dx in range(2) for dy in range(2) for dz in range(2))
DIRECTIONS = OFFSETS[1:]
BATCH = ("chip", "core")
OTHERS = ("brick", "chip")


def region_of(rank):
    return (rank // 4, rank // 2 % 2, rank % 2)


def neighbour_pairs(regions, direction, sign):
    grid = (regions // 4, 2, 2)
    pairs = []
    for dst in range(regions):
        spot = region_of(dst)
        src = tuple(spot[a] + sign * direction[a] for a in range(3))
        if all(0 <= src[a] < grid[a] for a in range(3)):
            pairs.append((4 * src[0] + 2 * src[1] + src[2], dst))
    return pairs


def exchange(piece, regions, direction, sign):
    pairs = neighbour_pairs(regions, direction, sign)
    if not pairs:
        return jnp.zeros_like(piece)
    return lax.ppermute(piece, "brick", pairs)


def halo_exchange(masked_piece, cot_piece, regions, direction):
    down = neighbour_pairs(regions, direction, 1)
    up = neighbour_pairs(regions, direction, -1)
    both = down + up
    sources = [a for a, _ in both]
    targets = [b for _, b in both]
    if not both or len(set(sources)) < len(both) or len(set(targets)) < len(both):
        return (
            exchange(masked_piece, regions, direction, 1),
            exchange(cot_piece, regions, direction, -1),
        )
    spot = region_of(lax.axis_index("brick"))
    grid = (regions // 4, 2, 2)
    sends_down = jnp.bool_(True)
    sends_up = jnp.bool_(True)
    for a in range(3):
        if direction[a]:
            sends_down = sends_down & (spot[a] >= 1)
            sends_up = sends_up & (spot[a] + 1 < grid[a])
    cut = masked_piece.size
    zero = jnp.zeros((), masked_piece.dtype)
    packed = jnp.concatenate(
        [
            jnp.where(sends_down, masked_piece.reshape(-1), zero),
            jnp.where(sends_up, cot_piece.reshape(-1), zero),
        ]
    )
    got = lax.ppermute(packed, "brick", both)
    return (got[:cut].reshape(masked_piece.shape), got[cut:].reshape(cot_piece.shape))


def all_reduce(half):
    devices = lax.axis_size("brick") * lax.axis_size("chip")
    lanes = half.shape[-1]
    rows = half.reshape(-1, lanes)
    size = rows.shape[0]
    chunk = -(-size // (devices * 8)) * 8
    rows = jnp.pad(rows, ((0, chunk * devices - size), (0, 0)))
    parts = lax.all_to_all(rows.reshape(devices, chunk, lanes), OTHERS, 0, 0, tiled=True)
    return parts.sum(axis=0), (devices, chunk, size, half.shape)


def all_spread(reduced, plan, riders):
    devices, chunk, size, shape = plan
    spread = jnp.broadcast_to(reduced[None], (devices,) + reduced.shape)
    half = lax.all_to_all(spread, OTHERS, 0, 0, tiled=True)
    half, riders = lax.optimization_barrier((half, riders))
    half = half.reshape(-1, reduced.shape[-1])[:size].reshape(shape)
    other = lax.ppermute(half, "core", [(0, 1), (1, 0)])
    core = lax.axis_index("core")
    whole = jnp.zeros((shape[0], 2) + shape[1:], half.dtype)
    whole = lax.dynamic_update_index_in_dim(whole, half, core, 1)
    whole = lax.dynamic_update_index_in_dim(whole, other, 1 - core, 1)
    return whole.reshape(shape[0], 2 * shape[1], shape[2]), riders


def body(coarse, coarse_mask, skip, fine_mask, up_weight, fine_grad):
    regions = lax.axis_size("brick")
    size_x, size_y, merged = coarse.shape[2:]
    channels_out = up_weight.shape[1]
    channels_in = up_weight.shape[2]
    size_z = merged // channels_in
    fine_x, fine_y, fine_merged = skip.shape[2:]
    fine_z = fine_merged // channels_out
    counts = (size_x, size_y, size_z)

    coarse_keep = coarse_mask.reshape(size_x, size_y, size_z, 1).astype(jnp.bfloat16)
    masked = coarse.reshape(size_x, size_y, size_z, channels_in) * coarse_keep
    fine_keep = fine_mask.reshape(fine_x, fine_y, fine_z, 1)
    cotangent = fine_grad.reshape(fine_x, fine_y, fine_z, channels_out) * fine_keep.astype(
        jnp.bfloat16
    )

    extended = masked
    widened = cotangent
    first_masked = (
        coarse.reshape(size_x, size_y, merged)[:, :, :channels_in]
        * coarse_keep[:, :, :1, 0]
    ).reshape(size_x, size_y, 1, channels_in)
    first_cot = (
        fine_grad.reshape(fine_x, fine_y, fine_merged)[:, :, (fine_z - 1) * channels_out :]
        * fine_keep[:, :, fine_z - 1 :, 0].astype(jnp.bfloat16)
    ).reshape(fine_x, fine_y, 1, channels_out)
    for axis in (2, 1, 0):
        direction = tuple(1 if other == axis else 0 for other in range(3))
        last = widened.shape[axis]
        faces = (
            lax.slice_in_dim(extended, 0, 1, axis=axis),
            lax.slice_in_dim(widened, last - 1, last, axis=axis),
        )
        if axis == 2:
            faces = (first_masked, first_cot)
        got_masked, got_cot = halo_exchange(*faces, regions, direction)
        extended = jnp.concatenate([extended, got_masked], axis=axis)
        widened = jnp.concatenate([got_cot, widened], axis=axis)
    full = lax.conv_general_dilated(
        widened[..., None],
        masked[..., None],
        (1, 1, 1),
        "VALID",
        rhs_dilation=(2, 2, 2),
        dimension_numbers=("XYZNC", "XYZOI", "XYZNC"),
        preferred_element_type=jnp.float32,
    ).reshape(27, channels_out, channels_in)
    core = lax.axis_index("core")
    share = channels_out // 2
    theirs = lax.dynamic_slice_in_dim(full, (1 - core) * share, share, axis=1)
    got = lax.ppermute(theirs, "core", [(0, 1), (1, 0)])
    grads = lax.dynamic_slice_in_dim(full, core * share, share, axis=1) + got
    grads, extended, weight_late, skip, fine_keep = lax.optimization_barrier(
        (grads, extended, up_weight, skip, fine_keep)
    )
    reduced, plan = all_reduce(grads)

    back = lax.conv_general_dilated(
        widened[None],
        up_weight.reshape((3, 3, 3, channels_out, channels_in)),
        (2, 2, 2),
        "VALID",
        dimension_numbers=("NXYZC", "XYZIO", "NXYZC"),
        preferred_element_type=jnp.float32,
    )[0]
    coarse_grad = (
        (back * coarse_keep.astype(jnp.float32)).astype(jnp.bfloat16).reshape(coarse.shape)
    )

    flipped = weight_late.reshape((3, 3, 3, channels_out, channels_in))[::-1, ::-1, ::-1]
    up = lax.conv_general_dilated(
        extended[None],
        flipped,
        (1, 1, 1),
        ((1, 0), (1, 0), (1, 0)),
        lhs_dilation=(2, 2, 2),
        dimension_numbers=("NXYZC", "XYZOI", "NXYZC"),
        preferred_element_type=jnp.float32,
    )[0]
    fine = fine_keep.astype(jnp.float32) * (
        skip.reshape(fine_x, fine_y, fine_z, channels_out).astype(jnp.float32) + up
    )
    fine_out = fine.astype(jnp.bfloat16).reshape(skip.shape)

    scale = 1.0 / math.sqrt(regions * lax.axis_size("chip") * lax.axis_size("core") * size_x * size_y * size_z)
    weight_grad, (fine_out, coarse_grad) = all_spread(
        reduced * scale, plan, (fine_out, coarse_grad)
    )
    return (fine_out, coarse_grad, weight_grad)


def solution(mesh):
    brick, batch = mesh.shape["brick"], mesh.shape["batch"]
    pairs = Mesh(
        mesh.devices.reshape(brick, batch // 2, 2), ("brick", "chip", "core")
    )
    in_specs = (
        P(BATCH, "brick", None, None, None),
        P(BATCH, "brick", None),
        P(BATCH, "brick", None, None, None),
        P(BATCH, "brick", None),
        P(),
        P(BATCH, "brick", None, None, None),
    )
    out_specs = (P(BATCH, "brick", None, None, None), P(BATCH, "brick", None, None, None), P())
    return jax.shard_map(body, mesh=pairs, in_specs=in_specs, out_specs=out_specs, check_vma=False)
```

```python
import math

import jax
import jax.numpy as jnp
from jax import lax
from jax.sharding import Mesh, PartitionSpec as P

OFFSETS = tuple((dx, dy, dz) for dx in range(2) for dy in range(2) for dz in range(2))
DIRECTIONS = OFFSETS[1:]
BATCH = ("chip", "core")
OTHERS = ("brick", "chip")


def region_of(rank):
    return (rank // 4, rank // 2 % 2, rank % 2)


def neighbour_pairs(regions, direction, sign):
    grid = (regions // 4, 2, 2)
    pairs = []
    for dst in range(regions):
        spot = region_of(dst)
        src = tuple(spot[a] + sign * direction[a] for a in range(3))
        if all(0 <= src[a] < grid[a] for a in range(3)):
            pairs.append((4 * src[0] + 2 * src[1] + src[2], dst))
    return pairs


def exchange(piece, regions, direction, sign):
    pairs = neighbour_pairs(regions, direction, sign)
    if not pairs:
        return jnp.zeros_like(piece)
    return lax.ppermute(piece, "brick", pairs)


def halo_exchange(masked_piece, cot_piece, regions, direction):
    down = neighbour_pairs(regions, direction, 1)
    up = neighbour_pairs(regions, direction, -1)
    both = down + up
    sources = [a for a, _ in both]
    targets = [b for _, b in both]
    if not both or len(set(sources)) < len(both) or len(set(targets)) < len(both):
        return (
            exchange(masked_piece, regions, direction, 1),
            exchange(cot_piece, regions, direction, -1),
        )
    spot = region_of(lax.axis_index("brick"))
    grid = (regions // 4, 2, 2)
    sends_down = jnp.bool_(True)
    sends_up = jnp.bool_(True)
    for a in range(3):
        if direction[a]:
            sends_down = sends_down & (spot[a] >= 1)
            sends_up = sends_up & (spot[a] + 1 < grid[a])
    cut = masked_piece.size
    zero = jnp.zeros((), masked_piece.dtype)
    packed = jnp.concatenate(
        [
            jnp.where(sends_down, masked_piece.reshape(-1), zero),
            jnp.where(sends_up, cot_piece.reshape(-1), zero),
        ]
    )
    got = lax.ppermute(packed, "brick", both)
    return (got[:cut].reshape(masked_piece.shape), got[cut:].reshape(cot_piece.shape))


def all_reduce(half):
    devices = lax.axis_size("brick") * lax.axis_size("chip")
    lanes = half.shape[-1]
    rows = half.reshape(-1, lanes)
    size = rows.shape[0]
    chunk = -(-size // (devices * 8)) * 8
    rows = jnp.pad(rows, ((0, chunk * devices - size), (0, 0)))
    parts = lax.all_to_all(rows.reshape(devices, chunk, lanes), OTHERS, 0, 0, tiled=True)
    return parts.sum(axis=0), (devices, chunk, size, half.shape)


def all_spread(reduced, plan, riders):
    devices, chunk, size, shape = plan
    spread = jnp.broadcast_to(reduced[None], (devices,) + reduced.shape)
    half = lax.all_to_all(spread, OTHERS, 0, 0, tiled=True)
    half, riders = lax.optimization_barrier((half, riders))
    half = half.reshape(-1, reduced.shape[-1])[:size].reshape(shape)
    other = lax.ppermute(half, "core", [(0, 1), (1, 0)])
    core = lax.axis_index("core")
    whole = jnp.zeros((shape[0], 2) + shape[1:], half.dtype)
    whole = lax.dynamic_update_index_in_dim(whole, half, core, 1)
    whole = lax.dynamic_update_index_in_dim(whole, other, 1 - core, 1)
    return whole.reshape(shape[0], 2 * shape[1], shape[2]), riders


def body(coarse, coarse_mask, skip, fine_mask, up_weight, fine_grad):
    regions = lax.axis_size("brick")
    size_x, size_y, merged = coarse.shape[2:]
    channels_out = up_weight.shape[1]
    channels_in = up_weight.shape[2]
    size_z = merged // channels_in
    fine_x, fine_y, fine_merged = skip.shape[2:]
    fine_z = fine_merged // channels_out
    counts = (size_x, size_y, size_z)

    coarse_keep = coarse_mask.reshape(size_x, size_y, size_z, 1).astype(jnp.bfloat16)
    masked = coarse.reshape(size_x, size_y, size_z, channels_in) * coarse_keep
    fine_keep = fine_mask.reshape(fine_x, fine_y, fine_z, 1)
    cotangent = fine_grad.reshape(fine_x, fine_y, fine_z, channels_out) * fine_keep.astype(
        jnp.bfloat16
    )

    extended = masked
    widened = cotangent
    for axis in (1, 2, 0):
        direction = tuple(1 if other == axis else 0 for other in range(3))
        last = widened.shape[axis]
        got_masked, got_cot = halo_exchange(
            lax.slice_in_dim(extended, 0, 1, axis=axis),
            lax.slice_in_dim(widened, last - 1, last, axis=axis),
            regions,
            direction,
        )
        extended = jnp.concatenate([extended, got_masked], axis=axis)
        widened = jnp.concatenate([got_cot, widened], axis=axis)
    full = lax.conv_general_dilated(
        widened[..., None],
        masked[..., None],
        (1, 1, 1),
        "VALID",
        rhs_dilation=(2, 2, 2),
        dimension_numbers=("XYZNC", "XYZOI", "XYZNC"),
        preferred_element_type=jnp.float32,
    ).reshape(27, channels_out, channels_in)
    core = lax.axis_index("core")
    share = channels_out // 2
    theirs = lax.dynamic_slice_in_dim(full, (1 - core) * share, share, axis=1)
    got = lax.ppermute(theirs, "core", [(0, 1), (1, 0)])
    grads = lax.dynamic_slice_in_dim(full, core * share, share, axis=1) + got
    grads, extended, weight_late, skip, fine_keep = lax.optimization_barrier(
        (grads, extended, up_weight, skip, fine_keep)
    )
    reduced, plan = all_reduce(grads)

    back = lax.conv_general_dilated(
        widened[None],
        up_weight.reshape((3, 3, 3, channels_out, channels_in)),
        (2, 2, 2),
        "VALID",
        dimension_numbers=("NXYZC", "XYZIO", "NXYZC"),
        preferred_element_type=jnp.float32,
    )[0]
    coarse_grad = (
        (back * coarse_keep.astype(jnp.float32)).astype(jnp.bfloat16).reshape(coarse.shape)
    )

    flipped = weight_late.reshape((3, 3, 3, channels_out, channels_in))[::-1, ::-1, ::-1]
    up = lax.conv_general_dilated(
        extended[None],
        flipped,
        (1, 1, 1),
        ((1, 0), (1, 0), (1, 0)),
        lhs_dilation=(2, 2, 2),
        dimension_numbers=("NXYZC", "XYZOI", "NXYZC"),
        preferred_element_type=jnp.float32,
    )[0]
    fine = fine_keep.astype(jnp.float32) * (
        skip.reshape(fine_x, fine_y, fine_z, channels_out).astype(jnp.float32) + up
    )
    fine_out = fine.astype(jnp.bfloat16).reshape(skip.shape)

    scale = 1.0 / math.sqrt(regions * lax.axis_size("chip") * lax.axis_size("core") * size_x * size_y * size_z)
    weight_grad, (fine_out, coarse_grad) = all_spread(
        reduced * scale, plan, (fine_out, coarse_grad)
    )
    return (fine_out, coarse_grad, weight_grad)


def solution(mesh):
    brick, batch = mesh.shape["brick"], mesh.shape["batch"]
    pairs = Mesh(
        mesh.devices.reshape(brick, batch // 2, 2), ("brick", "chip", "core")
    )
    in_specs = (
        P(BATCH, "brick", None, None, None),
        P(BATCH, "brick", None),
        P(BATCH, "brick", None, None, None),
        P(BATCH, "brick", None),
        P(),
        P(BATCH, "brick", None, None, None),
    )
    out_specs = (P(BATCH, "brick", None, None, None), P(BATCH, "brick", None, None, None), P())
    return jax.shard_map(body, mesh=pairs, in_specs=in_specs, out_specs=out_specs, check_vma=False)
```

```python
import math

import jax
import jax.numpy as jnp
from jax import lax
from jax.sharding import Mesh, PartitionSpec as P

OFFSETS = tuple((dx, dy, dz) for dx in range(2) for dy in range(2) for dz in range(2))
DIRECTIONS = OFFSETS[1:]
BATCH = ("chip", "core")
OTHERS = ("brick", "chip")


def region_of(rank):
    return (rank // 4, rank // 2 % 2, rank % 2)


def neighbour_pairs(regions, direction, sign):
    grid = (regions // 4, 2, 2)
    pairs = []
    for dst in range(regions):
        spot = region_of(dst)
        src = tuple(spot[a] + sign * direction[a] for a in range(3))
        if all(0 <= src[a] < grid[a] for a in range(3)):
            pairs.append((4 * src[0] + 2 * src[1] + src[2], dst))
    return pairs


def exchange(piece, regions, direction, sign):
    pairs = neighbour_pairs(regions, direction, sign)
    if not pairs:
        return jnp.zeros_like(piece)
    return lax.ppermute(piece, "brick", pairs)


def halo_exchange(masked_piece, cot_piece, regions, direction):
    down = neighbour_pairs(regions, direction, 1)
    up = neighbour_pairs(regions, direction, -1)
    both = down + up
    sources = [a for a, _ in both]
    targets = [b for _, b in both]
    if not both or len(set(sources)) < len(both) or len(set(targets)) < len(both):
        return (
            exchange(masked_piece, regions, direction, 1),
            exchange(cot_piece, regions, direction, -1),
        )
    spot = region_of(lax.axis_index("brick"))
    grid = (regions // 4, 2, 2)
    sends_down = jnp.bool_(True)
    sends_up = jnp.bool_(True)
    for a in range(3):
        if direction[a]:
            sends_down = sends_down & (spot[a] >= 1)
            sends_up = sends_up & (spot[a] + 1 < grid[a])
    cut = masked_piece.size
    zero = jnp.zeros((), masked_piece.dtype)
    packed = jnp.concatenate(
        [
            jnp.where(sends_down, masked_piece.reshape(-1), zero),
            jnp.where(sends_up, cot_piece.reshape(-1), zero),
        ]
    )
    got = lax.ppermute(packed, "brick", both)
    return (got[:cut].reshape(masked_piece.shape), got[cut:].reshape(cot_piece.shape))


def all_reduce(half):
    devices = lax.axis_size("brick") * lax.axis_size("chip")
    lanes = half.shape[-1]
    rows = half.reshape(-1, lanes)
    size = rows.shape[0]
    chunk = -(-size // (devices * 8)) * 8
    rows = jnp.pad(rows, ((0, chunk * devices - size), (0, 0)))
    parts = lax.all_to_all(rows.reshape(devices, chunk, lanes), OTHERS, 0, 0, tiled=True)
    return parts.sum(axis=0), (devices, chunk, size, half.shape)


def all_spread(reduced, plan, riders):
    devices, chunk, size, shape = plan
    spread = jnp.broadcast_to(reduced[None], (devices,) + reduced.shape)
    half = lax.all_to_all(spread, OTHERS, 0, 0, tiled=True)
    half, riders = lax.optimization_barrier((half, riders))
    half = half.reshape(-1, reduced.shape[-1])[:size].reshape(shape)
    other = lax.ppermute(half, "core", [(0, 1), (1, 0)])
    core = lax.axis_index("core")
    whole = jnp.zeros((shape[0], 2) + shape[1:], half.dtype)
    whole = lax.dynamic_update_index_in_dim(whole, half, core, 1)
    whole = lax.dynamic_update_index_in_dim(whole, other, 1 - core, 1)
    return whole.reshape(shape[0], 2 * shape[1], shape[2]), riders


def body(coarse, coarse_mask, skip, fine_mask, up_weight, fine_grad):
    regions = lax.axis_size("brick")
    size_x, size_y, merged = coarse.shape[2:]
    channels_out = up_weight.shape[1]
    channels_in = up_weight.shape[2]
    size_z = merged // channels_in
    fine_x, fine_y, fine_merged = skip.shape[2:]
    fine_z = fine_merged // channels_out
    counts = (size_x, size_y, size_z)

    coarse_keep = coarse_mask.reshape(size_x, size_y, size_z, 1).astype(jnp.bfloat16)
    masked = coarse.reshape(size_x, size_y, size_z, channels_in) * coarse_keep
    fine_keep = fine_mask.reshape(fine_x, fine_y, fine_z, 1)
    cotangent = fine_grad.reshape(fine_x, fine_y, fine_z, channels_out) * fine_keep.astype(
        jnp.bfloat16
    )

    extended = masked
    widened = cotangent
    for axis in (2, 1, 0):
        direction = tuple(1 if other == axis else 0 for other in range(3))
        last = widened.shape[axis]
        got_masked, got_cot = halo_exchange(
            lax.slice_in_dim(extended, 0, 1, axis=axis),
            lax.slice_in_dim(widened, last - 1, last, axis=axis),
            regions,
            direction,
        )
        extended = jnp.concatenate([extended, got_masked], axis=axis)
        widened = jnp.concatenate([got_cot, widened], axis=axis)
    full = lax.conv_general_dilated(
        widened[..., None],
        masked[..., None],
        (1, 1, 1),
        "VALID",
        rhs_dilation=(2, 2, 2),
        dimension_numbers=("XYZNC", "XYZOI", "XYZNC"),
        preferred_element_type=jnp.float32,
    ).reshape(27, channels_out, channels_in)
    core = lax.axis_index("core")
    share = channels_out // 2
    theirs = lax.dynamic_slice_in_dim(full, (1 - core) * share, share, axis=1)
    got = lax.ppermute(theirs, "core", [(0, 1), (1, 0)])
    grads = lax.dynamic_slice_in_dim(full, core * share, share, axis=1) + got
    grads, weight_late, skip, fine_keep = lax.optimization_barrier(
        (grads, up_weight, skip, fine_keep)
    )
    reduced, plan = all_reduce(grads)

    back = lax.conv_general_dilated(
        widened[None],
        up_weight.reshape((3, 3, 3, channels_out, channels_in)),
        (2, 2, 2),
        "VALID",
        dimension_numbers=("NXYZC", "XYZIO", "NXYZC"),
        preferred_element_type=jnp.float32,
    )[0]
    coarse_grad = (
        (back * coarse_keep.astype(jnp.float32)).astype(jnp.bfloat16).reshape(coarse.shape)
    )

    flipped = weight_late.reshape((3, 3, 3, channels_out, channels_in))[::-1, ::-1, ::-1]
    up = lax.conv_general_dilated(
        extended[None],
        flipped,
        (1, 1, 1),
        ((1, 0), (1, 0), (1, 0)),
        lhs_dilation=(2, 2, 2),
        dimension_numbers=("NXYZC", "XYZOI", "NXYZC"),
        preferred_element_type=jnp.float32,
    )[0]
    fine = fine_keep.astype(jnp.float32) * (
        skip.reshape(fine_x, fine_y, fine_z, channels_out).astype(jnp.float32) + up
    )
    fine_out = fine.astype(jnp.bfloat16).reshape(skip.shape)

    scale = 1.0 / math.sqrt(regions * lax.axis_size("chip") * lax.axis_size("core") * size_x * size_y * size_z)
    weight_grad, (fine_out, coarse_grad) = all_spread(
        reduced * scale, plan, (fine_out, coarse_grad)
    )
    return (fine_out, coarse_grad, weight_grad)


def solution(mesh):
    brick, batch = mesh.shape["brick"], mesh.shape["batch"]
    pairs = Mesh(
        mesh.devices.reshape(brick, batch // 2, 2), ("brick", "chip", "core")
    )
    in_specs = (
        P(BATCH, "brick", None, None, None),
        P(BATCH, "brick", None),
        P(BATCH, "brick", None, None, None),
        P(BATCH, "brick", None),
        P(),
        P(BATCH, "brick", None, None, None),
    )
    out_specs = (P(BATCH, "brick", None, None, None), P(BATCH, "brick", None, None, None), P())
    return jax.shard_map(body, mesh=pairs, in_specs=in_specs, out_specs=out_specs, check_vma=False)
```
